512 devices in a mesh: seq: 32 (over y, z_lo, core), head: 16 (over x, z_hi).
Axes of the slice: x: 4, y: 8, z: 8 (z_hi: 4, z_lo: 2; z = z_hi * 2 + z_lo), core: 2. Of those that a mesh axis runs over, the one named last changes fastest.
Arguments:
- queries: bfloat16 [65536, 64, 128], P(('seq', 'head')), may hold values from -6 to 6
- keys: bfloat16 [65536, 8, 128], P(('seq', 'head')), may hold values from -6 to 6
- values: bfloat16 [65536, 8, 128], P(('seq', 'head')), may hold values from -6 to 6
- block_lists: int32 [8, 512, 8], replicated, may hold values from 0 to 511, as said below
- block_counts: int32 [8, 512], replicated, may hold values from 1 to 8, as said below
Outputs:
- attended: bfloat16 [65536, 64, 128], P(('seq', 'head'))
The draws below stay inside these ranges and needn't reach their ends.
Inputs may be any that keep to these rules, and one draw needn't show every extreme that they name: block_lists[g, b, 0] is b. For 1 <= j < block_counts[g, b] the slot names a block of another seq shard (block c lies on shard c // 16), distinct within the row; slots from block_counts[g, b] on repeat b. Over the 16 rows of one seq shard and one head g, at most 4 read slots name blocks of any one other shard, and some pair of shards reaches 4 for every g. `block_counts`: for every head g, all rows of one seq shard have 8.
All inputs are finite; a program needn't handle non-finite values.
Results may differ from the reference program's by a relative error of at most 0.0049.
Values may be sent and summed in bfloat16 or wider, within the bound.
No kernel may reach another device: no remote copies, remote signals or barrier semaphores. Data moves between devices by JAX's collectives and lax.ppermute only.
A program may use at most 128 MiB of HBM per device.

```python
from functools import partial
import jax
import jax.numpy as jnp
from jax import lax

HQ = 64
KVH = 8
DH = 128
BLK = 128
MAXSEL = 8
TOKENS = 65536
QB = 16
NB = 512


def block_tables(key):
    shard_count = NB // QB
    entries = QB * (MAXSEL - 1)
    key_perm, key_start, key_hot, key_count = jax.random.split(key, 4)
    perm_keys = jax.random.split(key_perm, KVH * shard_count)

    def shuffled(single_key):
        return jax.random.permutation(single_key, entries)
    orders = jax.vmap(shuffled)(perm_keys).reshape(KVH, shard_count, entries).astype(jnp.int32)
    offset = 1 + orders % (shard_count - 1)
    rounds = orders // (shard_count - 1)
    target = jnp.arange(shard_count, dtype=jnp.int32)[None, :, None]
    owner_shard = (target + offset) % shard_count
    start_base = jax.random.randint(key_start, (KVH, shard_count, shard_count), 0, QB, dtype=jnp.int32)
    first_block = jnp.take_along_axis(start_base, owner_shard, axis=2)
    within = (first_block + rounds) % QB
    remote = (owner_shard * QB + within).reshape(KVH, NB, MAXSEL - 1)
    hot_shard = jax.random.randint(key_hot, (KVH, 1), 0, shard_count, dtype=jnp.int32)
    light_counts = jnp.minimum(jax.random.randint(key_count, (KVH, NB), 1, 6, dtype=jnp.int32), MAXSEL)
    shard_of = (jnp.arange(NB, dtype=jnp.int32) // QB)[None, :]
    counts = jnp.where(shard_of == hot_shard, MAXSEL, light_counts).astype(jnp.int32)
    slot_number = jnp.arange(1, MAXSEL, dtype=jnp.int32)
    own_block = jnp.broadcast_to(jnp.arange(NB, dtype=jnp.int32)[None, :, None], (KVH, NB, 1))
    remote = jnp.where(slot_number[None, None, :] < counts[:, :, None], remote, own_block)
    block_lists = jnp.concatenate([own_block, remote], axis=2).astype(jnp.int32)
    return (block_lists, counts)


def draw_block_lists(key, part):
    tables = block_tables(jax.random.fold_in(key, 11))
    return tables[0]


def draw_block_counts(key, part):
    tables = block_tables(jax.random.fold_in(key, 11))
    return tables[1]


def draw_queries(key, part):
    result = jnp.clip(jax.random.normal(jax.random.fold_in(key, 1), (TOKENS, HQ, DH), jnp.float32), -6.0, 6.0)
    return result.astype(jnp.bfloat16)


def draw_keys(key, part):
    result = jnp.clip(jax.random.normal(jax.random.fold_in(key, 2), (TOKENS, KVH, DH), jnp.float32), -6.0, 6.0)
    return result.astype(jnp.bfloat16)


def levels(key, shape, pieces, smallest, top_value):
    factor_of, own = 1.0, jax.random.fold_in(key, 6)
    for axis_at, shards_of in pieces:
        heights = jnp.exp(jax.random.uniform(jax.random.fold_in(own, axis_at), (shards_of,), jnp.float32, smallest / len(pieces), top_value / len(pieces)))
        factor_of = factor_of * jnp.repeat(heights, shape[axis_at] // shards_of).reshape([-1 if axis == axis_at else 1 for axis in range(len(shape))])
    return factor_of


def gaussian(rng, extent, scale, limit, cuts=(), kind=jnp.bfloat16):
    values = jax.random.normal(rng, extent, jnp.float32) * scale
    if len(cuts) > 0:
        values = levels(rng, extent, cuts, -0.22, 0.18) * values
    return jnp.clip(values, min=-limit, max=limit).astype(kind)


def setup_inputs(seed: int = 0) -> dict:
    seeds = jax.random.split(jax.random.key(seed), 6)
    queries = draw_queries(jax.random.fold_in(seeds[5], 71), 0)
    keys = draw_keys(jax.random.fold_in(seeds[5], 71), 0)
    values = gaussian(seeds[2], (TOKENS, KVH, DH), 1.0, 6.0, ((0, 512),))
    block_lists = draw_block_lists(jax.random.fold_in(seeds[5], 71), 0)
    block_counts = draw_block_counts(jax.random.fold_in(seeds[5], 71), 0)
    return dict(queries=queries, keys=keys, values=values, block_lists=block_lists, block_counts=block_counts)


NEG_FILL = -1.0e30


def attend_row(key_blocks, value_blocks, score_scale, inputs):
    query_row, slot_index, row_count = inputs
    slot_total = slot_index.shape[0]
    head_dim = key_blocks.shape[-1]
    key_rows = key_blocks[slot_index].reshape(slot_total * BLK, head_dim).astype(jnp.float32)
    value_rows = value_blocks[slot_index].reshape(slot_total * BLK, head_dim).astype(jnp.float32)
    scores = jnp.einsum("tgd,kd->tgk", query_row.astype(jnp.float32), key_rows) * score_scale
    allowed = (jnp.arange(slot_total * BLK, dtype=jnp.int32) // BLK) < row_count
    scores = jnp.where(allowed[None, None, :], scores, NEG_FILL)
    row_max = jnp.max(scores, axis=2, keepdims=True)
    weights = jnp.exp(scores - row_max)
    probs = (weights / jnp.sum(weights, axis=2, keepdims=True)).astype(jnp.bfloat16)
    return jnp.einsum("tgk,kd->tgd", probs.astype(jnp.float32), value_rows).astype(jnp.bfloat16)


def reference(queries, keys, values, block_lists, block_counts):
    head_dim = queries.shape[2]
    group_size = HQ // KVH
    score_scale = head_dim ** -0.5
    results = []
    for group_head in range(KVH):
        key_blocks = keys[:, group_head].reshape(NB, BLK, head_dim)
        value_blocks = values[:, group_head].reshape(NB, BLK, head_dim)
        query_rows = queries[:, group_head * group_size:(group_head + 1) * group_size].reshape(NB, BLK, group_size, head_dim)
        attended = lax.map(partial(attend_row, key_blocks, value_blocks, score_scale),
                           (query_rows, block_lists[group_head], block_counts[group_head]))
        results.append(attended.reshape(TOKENS, group_size, head_dim))
    return jnp.concatenate(results, axis=1)
```

```python
from functools import partial

import jax
import jax.numpy as jnp
from jax import lax
from jax.experimental import pallas as pl
from jax.experimental.pallas import tpu as pltpu
from jax.sharding import PartitionSpec as P

BLK = 128


NEG_FILL = -1e30


def attend_kernel(slot_ref, count_ref, query_ref, own_ref, recv_ref, out_ref, *, score_scale,
                  slot_total, qblocks):
    row = pl.program_id(0)
    query = query_ref[0]
    row_count = count_ref[row]
    scores = []
    values = []
    for slot in range(slot_total):
        if slot == 0:
            key = own_ref[0, row]
            value = own_ref[1, row]
        else:
            index = jnp.maximum(slot_ref[row, slot] - qblocks, 0)
            key = recv_ref[index, 0]
            value = recv_ref[index, 1]
        part = lax.dot_general(
            query, key, (((1,), (1,)), ((), ())), preferred_element_type=jnp.float32
        ) * score_scale
        if slot > 0:
            part = jnp.where(slot < row_count, part, NEG_FILL)
        scores.append(part)
        values.append(value)
    row_max = jnp.max(scores[0], axis=1, keepdims=True)
    for part in scores[1:]:
        row_max = jnp.maximum(row_max, jnp.max(part, axis=1, keepdims=True))
    weights = [jnp.exp(part - row_max) for part in scores]
    total = jnp.sum(weights[0], axis=1, keepdims=True)
    for part in weights[1:]:
        total = total + jnp.sum(part, axis=1, keepdims=True)
    inverse = 1.0 / total
    acc = None
    for part, value in zip(weights, values):
        probs = (part * inverse).astype(jnp.bfloat16)
        term = jnp.dot(probs, value, preferred_element_type=jnp.float32)
        acc = term if acc is None else acc + term
    out_ref[0] = acc.astype(out_ref.dtype)


def attend_all(query_rows, own_blocks, recv_blocks, slot_index, row_counts, score_scale):
    qblocks, rows, head_dim = query_rows.shape
    slot_total = slot_index.shape[1]
    kernel = partial(
        attend_kernel, score_scale=score_scale, slot_total=slot_total, qblocks=qblocks
    )
    return pl.pallas_call(
        kernel,
        out_shape=jax.ShapeDtypeStruct(query_rows.shape, query_rows.dtype),
        grid_spec=pltpu.PrefetchScalarGridSpec(
            num_scalar_prefetch=2,
            grid=(qblocks,),
            in_specs=[
                pl.BlockSpec((1, rows, head_dim), lambda r, s, c: (r, 0, 0)),
                pl.BlockSpec(own_blocks.shape, lambda r, s, c: (0, 0, 0, 0)),
                pl.BlockSpec(recv_blocks.shape, lambda r, s, c: (0, 0, 0, 0)),
            ],
            out_specs=pl.BlockSpec((1, rows, head_dim), lambda r, s, c: (r, 0, 0)),
        ),
        compiler_params=pltpu.CompilerParams(vmem_limit_bytes=100 * 1024 * 1024),
    )(slot_index, row_counts, query_rows, own_blocks, recv_blocks)


def make_plan(block_lists, block_counts, group_head, seq_index, shard_count, qblocks, capacity):
    slot_total = block_lists.shape[2]
    entries = qblocks * (slot_total - 1)
    row_lists = lax.dynamic_index_in_dim(block_lists, group_head, 0, keepdims=False)
    row_counts = lax.dynamic_index_in_dim(block_counts, group_head, 0, keepdims=False)
    slot_number = jnp.arange(1, slot_total, dtype=jnp.int32)
    live = (slot_number[None, :] < row_counts[:, None]).reshape(shard_count, entries)
    remote = row_lists[:, 1:].reshape(shard_count, entries)
    owner_shard = remote // qblocks
    within = remote % qblocks
    shard_ids = jnp.arange(shard_count, dtype=jnp.int32)
    hits = ((owner_shard[:, :, None] == shard_ids[None, None, :]) & live[:, :, None]).astype(
        jnp.int32
    )
    place = jnp.sum((jnp.cumsum(hits, axis=1) - hits) * hits, axis=2)
    mine = (live & (owner_shard == seq_index)).astype(jnp.int32)
    slot_match = (place[:, :, None] == jnp.arange(capacity, dtype=jnp.int32)[None, None, :]).astype(
        jnp.int32
    )
    chosen = jnp.sum(mine[:, :, None] * slot_match * within[:, :, None], axis=1)
    my_live = lax.dynamic_index_in_dim(live, seq_index, 0, keepdims=False)
    my_owner = lax.dynamic_index_in_dim(owner_shard, seq_index, 0, keepdims=False)
    my_place = jnp.minimum(lax.dynamic_index_in_dim(place, seq_index, 0, keepdims=False),
                           capacity - 1)
    remote_index = jnp.where(my_live, qblocks + my_owner * capacity + my_place, 0).reshape(
        qblocks, slot_total - 1
    )
    slot_index = jnp.concatenate(
        [jnp.arange(qblocks, dtype=jnp.int32)[:, None], remote_index], axis=1
    )
    my_counts = lax.dynamic_slice_in_dim(row_counts, seq_index * qblocks, qblocks, 0)
    return (chosen, slot_index, my_counts)


def on_device(queries, keys, values, block_lists, block_counts):
    head_count = lax.axis_size("head")
    shard_count = lax.axis_size("seq")
    head_index = lax.axis_index("head")
    seq_index = lax.axis_index("seq")
    kv_total = keys.shape[1]
    head_dim = keys.shape[2]
    share = max(1, head_count // kv_total)
    units = kv_total * share // head_count
    assert units == 1
    local_queries = lax.all_to_all(queries, "head", split_axis=1, concat_axis=0, tiled=True)
    seq_rows = local_queries.shape[0]
    qblocks = seq_rows // BLK
    group_size = local_queries.shape[1]
    slot_total = block_lists.shape[2]
    capacity = (qblocks * (slot_total - 1) + shard_count - 2) // (shard_count - 1)
    kv = jnp.stack([keys, values], axis=1)
    own_kv = lax.all_to_all(
        jnp.repeat(kv, share, axis=2), "head", split_axis=2, concat_axis=0, tiled=True
    )
    block_kv = own_kv.reshape(qblocks, BLK, 2, head_dim)
    group_head = head_index // share
    chosen, slot_index, my_counts = make_plan(
        block_lists, block_counts, group_head, seq_index, shard_count, qblocks, capacity
    )
    picked = jnp.transpose(block_kv[chosen], (0, 1, 3, 2, 4))
    recv = lax.all_to_all(picked, "seq", split_axis=0, concat_axis=0, tiled=True)
    recv_blocks = recv.reshape(shard_count * capacity, 2, BLK, head_dim)
    own_blocks = jnp.transpose(block_kv, (2, 0, 1, 3))
    score_scale = head_dim ** (-0.5)
    query_rows = local_queries.reshape(qblocks, BLK * group_size, head_dim)
    attended = attend_all(query_rows, own_blocks, recv_blocks, slot_index, my_counts, score_scale)
    outputs = attended.reshape(seq_rows, group_size, head_dim)
    return lax.all_to_all(outputs, "head", split_axis=0, concat_axis=1, tiled=True)


def solution(mesh):
    return jax.shard_map(
        on_device,
        mesh=mesh,
        in_specs=(
            P(("seq", "head"), None, None),
            P(("seq", "head"), None, None),
            P(("seq", "head"), None, None),
            P(),
            P(),
        ),
        out_specs=P(("seq", "head"), None, None),
        check_vma=False,
    )
```

```python
from functools import partial

import jax
import jax.numpy as jnp
from jax import lax
from jax.experimental import pallas as pl
from jax.experimental.pallas import tpu as pltpu
from jax.sharding import PartitionSpec as P

BLK = 128


NEG_FILL = -1e30


def attend_kernel(slot_ref, which_ref, count_ref, query_ref, own_ref, mine0_ref, mine1_ref,
                  peer0_ref, peer1_ref, out_ref, key_buf, value_buf, *, score_scale, slot_total):
    row = pl.program_id(0)
    query = query_ref[0]
    row_count = count_ref[row]
    sources = (mine0_ref, mine1_ref, peer0_ref, peer1_ref)
    for slot in range(1, slot_total):
        index = slot_ref[row, slot]
        which = which_ref[row, slot]
        for code, source in enumerate(sources):
            @pl.when(which == code)
            def _(source=source, slot=slot, index=index):
                key_buf[slot - 1] = source[index, 0]
                value_buf[slot - 1] = source[index, 1]
    scores = []
    values = []
    for slot in range(slot_total):
        if slot == 0:
            key = own_ref[0, row]
            value = own_ref[1, row]
        else:
            key = key_buf[slot - 1]
            value = value_buf[slot - 1]
        part = lax.dot_general(
            query, key, (((1,), (1,)), ((), ())), preferred_element_type=jnp.float32
        ) * score_scale
        if slot > 0:
            part = jnp.where(slot < row_count, part, NEG_FILL)
        scores.append(part)
        values.append(value)
    row_max = jnp.max(scores[0], axis=1, keepdims=True)
    for part in scores[1:]:
        row_max = jnp.maximum(row_max, jnp.max(part, axis=1, keepdims=True))
    weights = [jnp.exp(part - row_max) for part in scores]
    total = jnp.sum(weights[0], axis=1, keepdims=True)
    for part in weights[1:]:
        total = total + jnp.sum(part, axis=1, keepdims=True)
    inverse = 1.0 / total
    acc = None
    for part, value in zip(weights, values):
        probs = (part * inverse).astype(jnp.bfloat16)
        term = jnp.dot(probs, value, preferred_element_type=jnp.float32)
        acc = term if acc is None else acc + term
    out_ref[0] = acc.astype(out_ref.dtype)


def attend_all(query_rows, own_blocks, received, slot_index, slot_which, row_counts, score_scale):
    qblocks, rows, head_dim = query_rows.shape
    slot_total = slot_index.shape[1]
    kernel = partial(attend_kernel, score_scale=score_scale, slot_total=slot_total)
    whole = lambda shape: pl.BlockSpec(shape, lambda r, s, w, c: (0,) * len(shape))
    return pl.pallas_call(
        kernel,
        out_shape=jax.ShapeDtypeStruct(query_rows.shape, query_rows.dtype),
        grid_spec=pltpu.PrefetchScalarGridSpec(
            num_scalar_prefetch=3,
            grid=(qblocks,),
            in_specs=[
                pl.BlockSpec((1, rows, head_dim), lambda r, s, w, c: (r, 0, 0)),
                whole(own_blocks.shape),
            ]
            + [whole(part.shape) for part in received],
            out_specs=pl.BlockSpec((1, rows, head_dim), lambda r, s, w, c: (r, 0, 0)),
            scratch_shapes=[
                pltpu.VMEM((slot_total - 1, BLK, head_dim), own_blocks.dtype),
                pltpu.VMEM((slot_total - 1, BLK, head_dim), own_blocks.dtype),
            ],
        ),
        compiler_params=pltpu.CompilerParams(vmem_limit_bytes=100 * 1024 * 1024),
    )(slot_index, slot_which, row_counts, query_rows, own_blocks, *received)


def make_plan(block_lists, block_counts, group_head, seq_index, shard_count, qblocks, capacity):
    slot_total = block_lists.shape[2]
    entries = qblocks * (slot_total - 1)
    row_lists = lax.dynamic_index_in_dim(block_lists, group_head, 0, keepdims=False)
    row_counts = lax.dynamic_index_in_dim(block_counts, group_head, 0, keepdims=False)
    slot_number = jnp.arange(1, slot_total, dtype=jnp.int32)
    live = (slot_number[None, :] < row_counts[:, None]).reshape(shard_count, entries)
    remote = row_lists[:, 1:].reshape(shard_count, entries)
    owner_shard = remote // qblocks
    within = remote % qblocks
    shard_ids = jnp.arange(shard_count, dtype=jnp.int32)
    hits = ((owner_shard[:, :, None] == shard_ids[None, None, :]) & live[:, :, None]).astype(
        jnp.int32
    )
    place = jnp.sum((jnp.cumsum(hits, axis=1) - hits) * hits, axis=2)
    mine = (live & (owner_shard == seq_index)).astype(jnp.int32)
    slot_match = (place[:, :, None] == jnp.arange(capacity, dtype=jnp.int32)[None, None, :]).astype(
        jnp.int32
    )
    chosen = jnp.sum(mine[:, :, None] * slot_match * within[:, :, None], axis=1)
    my_live = lax.dynamic_index_in_dim(live, seq_index, 0, keepdims=False)
    my_owner = lax.dynamic_index_in_dim(owner_shard, seq_index, 0, keepdims=False)
    my_place = jnp.minimum(lax.dynamic_index_in_dim(place, seq_index, 0, keepdims=False),
                           capacity - 1)
    my_counts = lax.dynamic_slice_in_dim(row_counts, seq_index * qblocks, qblocks, 0)
    return (chosen, my_live, my_owner, my_place, my_counts)


def swap_halves(heads, inner):
    shape = heads.shape
    split = heads.reshape(shape[:1] + (2, inner, 6 - inner, 4) + shape[2:])
    return jnp.swapaxes(split, 2, 3).reshape(shape)


def on_device(queries, keys, values, block_lists, block_counts):
    head_count = lax.axis_size("head")
    shard_count = lax.axis_size("seq")
    head_index = lax.axis_index("head")
    seq_index = lax.axis_index("seq")
    kv_total = keys.shape[1]
    head_dim = keys.shape[2]
    assert head_count == 16 and kv_total == 8
    group_head = (head_index // 8) * 4 + head_index % 4
    half = (head_index // 4) % 2
    local_queries = lax.all_to_all(
        swap_halves(queries, 4), "head", split_axis=1, concat_axis=0, tiled=True
    )
    seq_rows = local_queries.shape[0]
    qblocks = seq_rows // BLK
    group_size = local_queries.shape[1]
    slot_total = block_lists.shape[2]
    capacity = (qblocks * (slot_total - 1) + shard_count - 2) // (shard_count - 1)
    assert capacity == 4
    kv = jnp.stack([keys, values], axis=1)
    kv = jnp.broadcast_to(
        kv.reshape(kv.shape[0], 2, 2, 1, 4, head_dim), (kv.shape[0], 2, 2, 2, 4, head_dim)
    ).reshape(kv.shape[0], 2, head_count, head_dim)
    own_kv = lax.all_to_all(kv, "head", split_axis=2, concat_axis=0, tiled=True)
    block_kv = own_kv.reshape(qblocks, BLK, 2, head_dim)
    chosen, my_live, my_owner, my_place, my_counts = make_plan(
        block_lists, block_counts, group_head, seq_index, shard_count, qblocks, capacity
    )
    partner = [(h, h ^ 4) for h in range(head_count)]
    mine = []
    peer = []
    for chunk in range(2):
        pick = lax.dynamic_index_in_dim(chosen, 2 * half + chunk, 1, keepdims=False)
        picked = jnp.transpose(block_kv[pick], (0, 2, 1, 3))
        got = lax.all_to_all(picked, "seq", split_axis=0, concat_axis=0, tiled=True)
        mine.append(got)
        peer.append(lax.ppermute(got, "head", partner))
    which = jnp.where(my_place // 2 == half, 0, 2) + my_place % 2
    slot_index = jnp.where(my_live, my_owner, 0).reshape(qblocks, slot_total - 1)
    slot_which = jnp.where(my_live, which, 0).reshape(qblocks, slot_total - 1)
    zero_col = jnp.zeros((qblocks, 1), jnp.int32)
    slot_index = jnp.concatenate([zero_col, slot_index], axis=1)
    slot_which = jnp.concatenate([zero_col, slot_which], axis=1)
    own_blocks = jnp.transpose(block_kv, (2, 0, 1, 3))
    score_scale = head_dim ** (-0.5)
    query_rows = local_queries.reshape(qblocks, BLK * group_size, head_dim)
    attended = attend_all(
        query_rows, own_blocks, mine + peer, slot_index, slot_which, my_counts, score_scale
    )
    outputs = attended.reshape(seq_rows, group_size, head_dim)
    back = lax.all_to_all(outputs, "head", split_axis=0, concat_axis=1, tiled=True)
    return swap_halves(back, 2)


def solution(mesh):
    return jax.shard_map(
        on_device,
        mesh=mesh,
        in_specs=(
            P(("seq", "head"), None, None),
            P(("seq", "head"), None, None),
            P(("seq", "head"), None, None),
            P(),
            P(),
        ),
        out_specs=P(("seq", "head"), None, None),
        check_vma=False,
    )
```

```python
from functools import partial

import jax
import jax.numpy as jnp
from jax import lax
from jax.experimental import pallas as pl
from jax.experimental.pallas import tpu as pltpu
from jax.sharding import PartitionSpec as P

BLK = 128


NEG_FILL = -1e30


def attend_kernel(slot_ref, which_ref, count_ref, query_ref, own_ref, mine0_ref, mine1_ref,
                  peer0_ref, peer1_ref, out_ref, key_buf, value_buf, *, score_scale, slot_total):
    row = pl.program_id(0)
    query = query_ref[0]
    row_count = count_ref[row]
    sources = (mine0_ref, mine1_ref, peer0_ref, peer1_ref)
    for slot in range(1, slot_total):
        index = slot_ref[row, slot]
        which = which_ref[row, slot]
        for code, source in enumerate(sources):
            @pl.when(which == code)
            def _(source=source, slot=slot, index=index):
                key_buf[slot - 1] = source[index, 0]
                value_buf[slot - 1] = source[index, 1]
    scores = []
    values = []
    for slot in range(slot_total):
        if slot == 0:
            key = own_ref[0, row]
            value = own_ref[1, row]
        else:
            key = key_buf[slot - 1]
            value = value_buf[slot - 1]
        part = lax.dot_general(
            query, key, (((1,), (1,)), ((), ())), preferred_element_type=jnp.float32
        ) * score_scale
        if slot > 0:
            part = jnp.where(slot < row_count, part, NEG_FILL)
        scores.append(part)
        values.append(value)
    row_max = jnp.max(scores[0], axis=1, keepdims=True)
    for part in scores[1:]:
        row_max = jnp.maximum(row_max, jnp.max(part, axis=1, keepdims=True))
    weights = [jnp.exp(part - row_max) for part in scores]
    total = jnp.sum(weights[0], axis=1, keepdims=True)
    for part in weights[1:]:
        total = total + jnp.sum(part, axis=1, keepdims=True)
    inverse = 1.0 / total
    acc = None
    for part, value in zip(weights, values):
        probs = (part * inverse).astype(jnp.bfloat16)
        term = jnp.dot(probs, value, preferred_element_type=jnp.float32)
        acc = term if acc is None else acc + term
    out_ref[0] = acc.astype(out_ref.dtype)


def attend_all(query_rows, own_blocks, received, slot_index, slot_which, row_counts, score_scale):
    qblocks, rows, head_dim = query_rows.shape
    slot_total = slot_index.shape[1]
    kernel = partial(attend_kernel, score_scale=score_scale, slot_total=slot_total)
    whole = lambda shape: pl.BlockSpec(shape, lambda r, s, w, c: (0,) * len(shape))
    return pl.pallas_call(
        kernel,
        out_shape=jax.ShapeDtypeStruct(query_rows.shape, query_rows.dtype),
        grid_spec=pltpu.PrefetchScalarGridSpec(
            num_scalar_prefetch=3,
            grid=(qblocks,),
            in_specs=[
                pl.BlockSpec((1, rows, head_dim), lambda r, s, w, c: (r, 0, 0)),
                whole(own_blocks.shape),
            ]
            + [whole(part.shape) for part in received],
            out_specs=pl.BlockSpec((1, rows, head_dim), lambda r, s, w, c: (r, 0, 0)),
            scratch_shapes=[
                pltpu.VMEM((slot_total - 1, BLK, head_dim), own_blocks.dtype),
                pltpu.VMEM((slot_total - 1, BLK, head_dim), own_blocks.dtype),
            ],
        ),
        compiler_params=pltpu.CompilerParams(vmem_limit_bytes=100 * 1024 * 1024),
    )(slot_index, slot_which, row_counts, query_rows, own_blocks, *received)


def make_plan(block_lists, block_counts, group_head, seq_index, shard_count, qblocks, capacity):
    slot_total = block_lists.shape[2]
    entries = qblocks * (slot_total - 1)
    row_lists = lax.dynamic_index_in_dim(block_lists, group_head, 0, keepdims=False)
    row_counts = lax.dynamic_index_in_dim(block_counts, group_head, 0, keepdims=False)
    slot_number = jnp.arange(1, slot_total, dtype=jnp.int32)
    live = (slot_number[None, :] < row_counts[:, None]).reshape(shard_count, entries)
    remote = row_lists[:, 1:].reshape(shard_count, entries)
    owner_shard = remote // qblocks
    within = remote % qblocks
    shard_ids = jnp.arange(shard_count, dtype=jnp.int32)
    hits = ((owner_shard[:, :, None] == shard_ids[None, None, :]) & live[:, :, None]).astype(
        jnp.int32
    )
    place = jnp.sum((jnp.cumsum(hits, axis=1) - hits) * hits, axis=2)
    mine = (live & (owner_shard == seq_index)).astype(jnp.int32)
    slot_match = (place[:, :, None] == jnp.arange(capacity, dtype=jnp.int32)[None, None, :]).astype(
        jnp.int32
    )
    chosen = jnp.sum(mine[:, :, None] * slot_match * within[:, :, None], axis=1)
    my_live = lax.dynamic_index_in_dim(live, seq_index, 0, keepdims=False)
    my_owner = lax.dynamic_index_in_dim(owner_shard, seq_index, 0, keepdims=False)
    my_place = jnp.minimum(lax.dynamic_index_in_dim(place, seq_index, 0, keepdims=False),
                           capacity - 1)
    my_counts = lax.dynamic_slice_in_dim(row_counts, seq_index * qblocks, qblocks, 0)
    return (chosen, my_live, my_owner, my_place, my_counts)


def swap_halves(heads, inner):
    shape = heads.shape
    split = heads.reshape(shape[:1] + (2, inner, 6 - inner, 4) + shape[2:])
    return jnp.swapaxes(split, 2, 3).reshape(shape)


def on_device(queries, keys, values, block_lists, block_counts):
    head_count = lax.axis_size("head")
    shard_count = lax.axis_size("seq")
    head_index = lax.axis_index("head")
    seq_index = lax.axis_index("seq")
    kv_total = keys.shape[1]
    head_dim = keys.shape[2]
    assert head_count == 16 and kv_total == 8
    group_head = (head_index // 8) * 4 + head_index % 4
    half = (head_index // 4) % 2
    seq_rows = queries.shape[0] * head_count
    qblocks = seq_rows // BLK
    group_size = queries.shape[1] // head_count
    slot_total = block_lists.shape[2]
    capacity = (qblocks * (slot_total - 1) + shard_count - 2) // (shard_count - 1)
    assert capacity == 4
    kv = jnp.stack([keys, values], axis=1)
    kv = jnp.broadcast_to(
        kv.reshape(kv.shape[0], 2, 2, 1, 4, head_dim), (kv.shape[0], 2, 2, 2, 4, head_dim)
    ).reshape(kv.shape[0], 2, head_count, head_dim)
    own_kv = lax.all_to_all(kv, "head", split_axis=2, concat_axis=0, tiled=True)
    block_kv = own_kv.reshape(qblocks, BLK, 2, head_dim)
    chosen, my_live, my_owner, my_place, my_counts = make_plan(
        block_lists, block_counts, group_head, seq_index, shard_count, qblocks, capacity
    )
    partner = [(h, h ^ 4) for h in range(head_count)]
    mine = []
    peer = []
    for chunk in range(2):
        pick = lax.dynamic_index_in_dim(chosen, 2 * half + chunk, 1, keepdims=False)
        picked = jnp.transpose(block_kv[pick], (0, 2, 1, 3))
        if chunk == 1:
            local_queries = lax.all_to_all(
                swap_halves(queries, 4), "head", split_axis=1, concat_axis=0, tiled=True
            )
            local_queries, picked = lax.optimization_barrier((local_queries, picked))
        got = lax.all_to_all(picked, "seq", split_axis=0, concat_axis=0, tiled=True)
        mine.append(got)
        peer.append(lax.ppermute(got, "head", partner))
    which = jnp.where(my_place // 2 == half, 0, 2) + my_place % 2
    slot_index = jnp.where(my_live, my_owner, 0).reshape(qblocks, slot_total - 1)
    slot_which = jnp.where(my_live, which, 0).reshape(qblocks, slot_total - 1)
    zero_col = jnp.zeros((qblocks, 1), jnp.int32)
    slot_index = jnp.concatenate([zero_col, slot_index], axis=1)
    slot_which = jnp.concatenate([zero_col, slot_which], axis=1)
    own_blocks = jnp.transpose(block_kv, (2, 0, 1, 3))
    score_scale = head_dim ** (-0.5)
    query_rows = local_queries.reshape(qblocks, BLK * group_size, head_dim)
    attended = attend_all(
        query_rows, own_blocks, mine + peer, slot_index, slot_which, my_counts, score_scale
    )
    outputs = attended.reshape(seq_rows, group_size, head_dim)
    back = lax.all_to_all(outputs, "head", split_axis=0, concat_axis=1, tiled=True)
    return swap_halves(back, 2)


def solution(mesh):
    return jax.shard_map(
        on_device,
        mesh=mesh,
        in_specs=(
            P(("seq", "head"), None, None),
            P(("seq", "head"), None, None),
            P(("seq", "head"), None, None),
            P(),
            P(),
        ),
        out_specs=P(("seq", "head"), None, None),
        check_vma=False,
    )
```

```python
from functools import partial

import jax
import jax.numpy as jnp
from jax import lax
from jax.experimental import pallas as pl
from jax.experimental.pallas import tpu as pltpu
from jax.sharding import PartitionSpec as P

BLK = 128
HEAD_SPLIT = 2


NEG_FILL = -1e30


def attend_kernel(slot_ref, which_ref, count_ref, query_ref, own_ref, mine0_ref, mine1_ref,
                  peer0_ref, peer1_ref, out_ref, block_buf, *, score_scale, slot_total, heads):
    row = pl.program_id(0)
    head_dim = block_buf.shape[2] // 2
    query = query_ref[...]
    query = jnp.concatenate(
        [query[:, h * head_dim:(h + 1) * head_dim] for h in range(heads)], axis=0
    )
    row_count = count_ref[row]
    sources = (mine0_ref, mine1_ref, peer0_ref, peer1_ref)
    for slot in range(1, slot_total):
        index = slot_ref[row, slot]
        which = which_ref[row, slot]
        for code, source in enumerate(sources):
            @pl.when(which == code)
            def _(source=source, slot=slot, index=index):
                block_buf[slot - 1] = source[index]
    scores = []
    values = []
    for slot in range(slot_total):
        block = own_ref[row] if slot == 0 else block_buf[slot - 1]
        key = block[:, :head_dim]
        value = block[:, head_dim:]
        part = lax.dot_general(
            query, key, (((1,), (1,)), ((), ())), preferred_element_type=jnp.float32
        ) * score_scale
        if slot > 0:
            part = jnp.where(slot < row_count, part, NEG_FILL)
        scores.append(part)
        values.append(value)
    row_max = jnp.max(scores[0], axis=1, keepdims=True)
    for part in scores[1:]:
        row_max = jnp.maximum(row_max, jnp.max(part, axis=1, keepdims=True))
    weights = [jnp.exp(part - row_max) for part in scores]
    total = jnp.sum(weights[0], axis=1, keepdims=True)
    for part in weights[1:]:
        total = total + jnp.sum(part, axis=1, keepdims=True)
    inverse = 1.0 / total
    acc = None
    for part, value in zip(weights, values):
        probs = (part * inverse).astype(jnp.bfloat16)
        term = jnp.dot(probs, value, preferred_element_type=jnp.float32)
        acc = term if acc is None else acc + term
    tokens = query_ref.shape[0]
    for h in range(heads):
        out_ref[:, h * head_dim:(h + 1) * head_dim] = acc[h * tokens:(h + 1) * tokens].astype(
            out_ref.dtype
        )


def attend_all(local_queries, column, width, own_blocks, received, slot_index, slot_which,
               row_counts, score_scale):
    seq_rows = local_queries.shape[0]
    qblocks, _, pair_dim = own_blocks.shape
    head_dim = pair_dim // 2
    slot_total = slot_index.shape[1]
    kernel = partial(
        attend_kernel, score_scale=score_scale, slot_total=slot_total, heads=width // head_dim
    )
    whole = lambda shape: pl.BlockSpec(shape, lambda r, s, w, c: (0,) * len(shape))
    return pl.pallas_call(
        kernel,
        out_shape=jax.ShapeDtypeStruct((seq_rows, width), local_queries.dtype),
        grid_spec=pltpu.PrefetchScalarGridSpec(
            num_scalar_prefetch=3,
            grid=(qblocks,),
            in_specs=[
                pl.BlockSpec((BLK, width), lambda r, s, w, c: (r, column)),
                whole(own_blocks.shape),
            ]
            + [whole(part.shape) for part in received],
            out_specs=pl.BlockSpec((BLK, width), lambda r, s, w, c: (r, 0)),
            scratch_shapes=[pltpu.VMEM((slot_total - 1, BLK, pair_dim), own_blocks.dtype)],
        ),
        compiler_params=pltpu.CompilerParams(vmem_limit_bytes=100 * 1024 * 1024),
    )(slot_index, slot_which, row_counts, local_queries, own_blocks, *received)


def make_plan(block_lists, block_counts, group_head, seq_index, shard_count, qblocks, capacity):
    slot_total = block_lists.shape[2]
    entries = qblocks * (slot_total - 1)
    row_lists = lax.dynamic_index_in_dim(block_lists, group_head, 0, keepdims=False)
    row_counts = lax.dynamic_index_in_dim(block_counts, group_head, 0, keepdims=False)
    slot_number = jnp.arange(1, slot_total, dtype=jnp.int32)
    live = (slot_number[None, :] < row_counts[:, None]).reshape(shard_count, entries)
    remote = row_lists[:, 1:].reshape(shard_count, entries)
    owner_shard = remote // qblocks
    within = remote % qblocks
    shard_ids = jnp.arange(shard_count, dtype=jnp.int32)
    hits = ((owner_shard[:, :, None] == shard_ids[None, None, :]) & live[:, :, None]).astype(
        jnp.int32
    )
    place = jnp.sum((jnp.cumsum(hits, axis=1) - hits) * hits, axis=2)
    mine = (live & (owner_shard == seq_index)).astype(jnp.int32)
    slot_match = (place[:, :, None] == jnp.arange(capacity, dtype=jnp.int32)[None, None, :]).astype(
        jnp.int32
    )
    chosen = jnp.sum(mine[:, :, None] * slot_match * within[:, :, None], axis=1)
    my_live = lax.dynamic_index_in_dim(live, seq_index, 0, keepdims=False)
    my_owner = lax.dynamic_index_in_dim(owner_shard, seq_index, 0, keepdims=False)
    my_place = jnp.minimum(lax.dynamic_index_in_dim(place, seq_index, 0, keepdims=False),
                           capacity - 1)
    my_counts = lax.dynamic_slice_in_dim(row_counts, seq_index * qblocks, qblocks, 0)
    return (chosen, my_live, my_owner, my_place, my_counts)


def swap_halves(heads, inner):
    shape = heads.shape
    split = heads.reshape(shape[:1] + (2, inner, 6 - inner, 4) + shape[2:])
    return jnp.swapaxes(split, 2, 3).reshape(shape)


def on_device(queries, keys, values, block_lists, block_counts):
    head_count = lax.axis_size("head")
    shard_count = lax.axis_size("seq")
    head_index = lax.axis_index("head")
    seq_index = lax.axis_index("seq")
    tokens, query_heads, head_dim = queries.shape
    kv_total = keys.shape[1]
    assert head_count == 16 and kv_total == 8
    group_head = (head_index // 8) * 4 + head_index % 4
    half = (head_index // 4) % 2
    seq_rows = tokens * head_count
    qblocks = seq_rows // BLK
    group_size = query_heads // head_count
    slot_total = block_lists.shape[2]
    capacity = (qblocks * (slot_total - 1) + shard_count - 2) // (shard_count - 1)
    assert capacity == 4
    kv = jnp.concatenate([keys, values], axis=2)
    kv = jnp.broadcast_to(
        kv.reshape(tokens, 2, 1, 4, 2 * head_dim), (tokens, 2, 2, 4, 2 * head_dim)
    ).reshape(tokens, head_count, 2 * head_dim)
    own_kv = lax.all_to_all(kv, "head", split_axis=1, concat_axis=0, tiled=True)
    own_blocks = own_kv.reshape(qblocks, BLK, 2 * head_dim)
    chosen, my_live, my_owner, my_place, my_counts = make_plan(
        block_lists, block_counts, group_head, seq_index, shard_count, qblocks, capacity
    )
    partner = [(h, h ^ 4) for h in range(head_count)]
    mine = []
    peer = []
    for chunk in range(2):
        pick = lax.dynamic_index_in_dim(chosen, 2 * half + chunk, 1, keepdims=False)
        picked = own_blocks[pick]
        if chunk == 1:
            spread = swap_halves(queries, 4).reshape(tokens, head_count, group_size * head_dim)
            local_queries = lax.all_to_all(spread, "head", split_axis=1, concat_axis=0, tiled=True)
            local_queries, picked = lax.optimization_barrier((local_queries, picked))
        got = lax.all_to_all(picked, "seq", split_axis=0, concat_axis=0, tiled=True)
        mine.append(got)
        peer.append(lax.ppermute(got, "head", partner))
    local_queries = local_queries.reshape(seq_rows, group_size * head_dim)
    which = jnp.where(my_place // 2 == half, 0, 2) + my_place % 2
    slot_index = jnp.where(my_live, my_owner, 0).reshape(qblocks, slot_total - 1)
    slot_which = jnp.where(my_live, which, 0).reshape(qblocks, slot_total - 1)
    zero_col = jnp.zeros((qblocks, 1), jnp.int32)
    slot_index = jnp.concatenate([zero_col, slot_index], axis=1)
    slot_which = jnp.concatenate([zero_col, slot_which], axis=1)
    score_scale = head_dim ** (-0.5)
    pieces = []
    width = group_size * head_dim // HEAD_SPLIT
    for column in range(HEAD_SPLIT):
        attended = attend_all(
            local_queries, column, width, own_blocks, mine + peer, slot_index, slot_which,
            my_counts, score_scale
        )
        back = lax.all_to_all(
            attended.reshape(seq_rows, 1, width), "head", split_axis=0, concat_axis=1, tiled=True
        )
        pieces.append(back)
    back = jnp.concatenate(pieces, axis=2).reshape(tokens, query_heads, head_dim)
    return swap_halves(back, 2)


def solution(mesh):
    return jax.shard_map(
        on_device,
        mesh=mesh,
        in_specs=(
            P(("seq", "head"), None, None),
            P(("seq", "head"), None, None),
            P(("seq", "head"), None, None),
            P(),
            P(),
        ),
        out_specs=P(("seq", "head"), None, None),
        check_vma=False,
    )
```

```python
from functools import partial

import jax
import jax.numpy as jnp
from jax import lax
from jax.experimental import pallas as pl
from jax.experimental.pallas import tpu as pltpu
from jax.sharding import PartitionSpec as P

BLK = 128


NEG_FILL = -1e30


def attend_kernel(slot_ref, which_ref, count_ref, query_ref, own_ref, mine0_ref, mine1_ref,
                  peer0_ref, peer1_ref, out_ref, block_buf, *, score_scale, slot_total, heads):
    row = pl.program_id(0)
    head_dim = block_buf.shape[2] // 2
    query = query_ref[...]
    query = jnp.concatenate(
        [query[:, h * head_dim:(h + 1) * head_dim] for h in range(heads)], axis=0
    )
    row_count = count_ref[row]
    sources = (mine0_ref, mine1_ref, peer0_ref, peer1_ref)
    for slot in range(1, slot_total):
        index = slot_ref[row, slot]
        which = which_ref[row, slot]
        for code, source in enumerate(sources):
            @pl.when(which == code)
            def _(source=source, slot=slot, index=index):
                block_buf[slot - 1] = source[index]
    scores = []
    values = []
    for slot in range(slot_total):
        block = own_ref[row] if slot == 0 else block_buf[slot - 1]
        key = block[:, :head_dim]
        value = block[:, head_dim:]
        part = lax.dot_general(
            query, key, (((1,), (1,)), ((), ())), preferred_element_type=jnp.float32
        ) * score_scale
        if slot > 0:
            part = jnp.where(slot < row_count, part, NEG_FILL)
        scores.append(part)
        values.append(value)
    row_max = jnp.max(scores[0], axis=1, keepdims=True)
    for part in scores[1:]:
        row_max = jnp.maximum(row_max, jnp.max(part, axis=1, keepdims=True))
    weights = [jnp.exp(part - row_max) for part in scores]
    total = jnp.sum(weights[0], axis=1, keepdims=True)
    for part in weights[1:]:
        total = total + jnp.sum(part, axis=1, keepdims=True)
    inverse = 1.0 / total
    acc = None
    for part, value in zip(weights, values):
        probs = (part * inverse).astype(jnp.bfloat16)
        term = jnp.dot(probs, value, preferred_element_type=jnp.float32)
        acc = term if acc is None else acc + term
    tokens = query_ref.shape[0]
    for h in range(heads):
        out_ref[:, h * head_dim:(h + 1) * head_dim] = acc[h * tokens:(h + 1) * tokens].astype(
            out_ref.dtype
        )


def attend_all(local_queries, column, width, own_blocks, received, slot_index, slot_which,
               row_counts, score_scale):
    seq_rows = local_queries.shape[0]
    qblocks, _, pair_dim = own_blocks.shape
    head_dim = pair_dim // 2
    slot_total = slot_index.shape[1]
    kernel = partial(
        attend_kernel, score_scale=score_scale, slot_total=slot_total, heads=width // head_dim
    )
    whole = lambda shape: pl.BlockSpec(shape, lambda r, s, w, c: (0,) * len(shape))
    return pl.pallas_call(
        kernel,
        out_shape=jax.ShapeDtypeStruct((seq_rows, width), local_queries.dtype),
        grid_spec=pltpu.PrefetchScalarGridSpec(
            num_scalar_prefetch=3,
            grid=(qblocks,),
            in_specs=[
                pl.BlockSpec((BLK, width), lambda r, s, w, c: (r, column)),
                whole(own_blocks.shape),
            ]
            + [whole(part.shape) for part in received],
            out_specs=pl.BlockSpec((BLK, width), lambda r, s, w, c: (r, 0)),
            scratch_shapes=[pltpu.VMEM((slot_total - 1, BLK, pair_dim), own_blocks.dtype)],
        ),
        compiler_params=pltpu.CompilerParams(vmem_limit_bytes=100 * 1024 * 1024),
    )(slot_index, slot_which, row_counts, local_queries, own_blocks, *received)


def make_plan(block_lists, block_counts, group_head, seq_index, shard_count, qblocks, capacity):
    slot_total = block_lists.shape[2]
    entries = qblocks * (slot_total - 1)
    row_lists = lax.dynamic_index_in_dim(block_lists, group_head, 0, keepdims=False)
    row_counts = lax.dynamic_index_in_dim(block_counts, group_head, 0, keepdims=False)
    slot_number = jnp.arange(1, slot_total, dtype=jnp.int32)
    live = (slot_number[None, :] < row_counts[:, None]).reshape(shard_count, entries)
    remote = row_lists[:, 1:].reshape(shard_count, entries)
    owner_shard = remote // qblocks
    within = remote % qblocks
    shard_ids = jnp.arange(shard_count, dtype=jnp.int32)
    hits = ((owner_shard[:, :, None] == shard_ids[None, None, :]) & live[:, :, None]).astype(
        jnp.int32
    )
    place = jnp.sum((jnp.cumsum(hits, axis=1) - hits) * hits, axis=2)
    mine = (live & (owner_shard == seq_index)).astype(jnp.int32)
    slot_match = (place[:, :, None] == jnp.arange(capacity, dtype=jnp.int32)[None, None, :]).astype(
        jnp.int32
    )
    chosen = jnp.sum(mine[:, :, None] * slot_match * within[:, :, None], axis=1)
    my_live = lax.dynamic_index_in_dim(live, seq_index, 0, keepdims=False)
    my_owner = lax.dynamic_index_in_dim(owner_shard, seq_index, 0, keepdims=False)
    my_place = jnp.minimum(lax.dynamic_index_in_dim(place, seq_index, 0, keepdims=False),
                           capacity - 1)
    my_counts = lax.dynamic_slice_in_dim(row_counts, seq_index * qblocks, qblocks, 0)
    return (chosen, my_live, my_owner, my_place, my_counts)


def on_device(queries, keys, values, block_lists, block_counts):
    head_count = lax.axis_size("head")
    shard_count = lax.axis_size("seq")
    head_index = lax.axis_index("head")
    seq_index = lax.axis_index("seq")
    tokens, query_heads, head_dim = queries.shape
    kv_total = keys.shape[1]
    assert head_count == 16 and kv_total == 8
    group_head = (head_index // 8) * 4 + head_index % 4
    half = (head_index // 4) % 2
    seq_rows = tokens * head_count
    qblocks = seq_rows // BLK
    group_size = query_heads // head_count
    slot_total = block_lists.shape[2]
    capacity = (qblocks * (slot_total - 1) + shard_count - 2) // (shard_count - 1)
    assert capacity == 4
    kv = jnp.concatenate([keys, values], axis=2)
    kv = jnp.transpose(kv.reshape(tokens, 2, 1, 4, 2 * head_dim), (1, 2, 3, 0, 4))
    kv = jnp.broadcast_to(kv, (2, 2, 4, tokens, 2 * head_dim))
    kv = kv.reshape(head_count, tokens, 2 * head_dim)
    own_blocks = lax.all_to_all(kv, "head", split_axis=0, concat_axis=0, tiled=True)
    chosen, my_live, my_owner, my_place, my_counts = make_plan(
        block_lists, block_counts, group_head, seq_index, shard_count, qblocks, capacity
    )
    partner = [(h, h ^ 4) for h in range(head_count)]
    mine = []
    peer = []
    for chunk in range(2):
        pick = lax.dynamic_index_in_dim(chosen, 2 * half + chunk, 1, keepdims=False)
        picked = own_blocks[pick]
        if chunk == 1:
            spread = jnp.transpose(
                queries.reshape(tokens, 2, 4, 2, group_size, head_dim), (1, 3, 2, 0, 4, 5)
            ).reshape(head_count, tokens, group_size * head_dim)
            local_queries = lax.all_to_all(spread, "head", split_axis=0, concat_axis=0, tiled=True)
            local_queries, picked = lax.optimization_barrier((local_queries, picked))
        got = lax.all_to_all(picked, "seq", split_axis=0, concat_axis=0, tiled=True)
        mine.append(got)
        peer.append(lax.ppermute(got, "head", partner))
    local_queries = local_queries.reshape(seq_rows, group_size * head_dim)
    which = jnp.where(my_place // 2 == half, 0, 2) + my_place % 2
    slot_index = jnp.where(my_live, my_owner, 0).reshape(qblocks, slot_total - 1)
    slot_which = jnp.where(my_live, which, 0).reshape(qblocks, slot_total - 1)
    zero_col = jnp.zeros((qblocks, 1), jnp.int32)
    slot_index = jnp.concatenate([zero_col, slot_index], axis=1)
    slot_which = jnp.concatenate([zero_col, slot_which], axis=1)
    score_scale = head_dim ** (-0.5)
    width = group_size * head_dim
    attended = attend_all(
        local_queries, 0, width, own_blocks, mine + peer, slot_index, slot_which,
        my_counts, score_scale
    )
    back = lax.all_to_all(
        attended.reshape(head_count, tokens, width), "head", split_axis=0, concat_axis=0,
        tiled=True
    )
    back = jnp.transpose(back.reshape(2, 2, 4, tokens, group_size, head_dim), (3, 0, 2, 1, 4, 5))
    return back.reshape(tokens, query_heads, head_dim)


def solution(mesh):
    return jax.shard_map(
        on_device,
        mesh=mesh,
        in_specs=(
            P(("seq", "head"), None, None),
            P(("seq", "head"), None, None),
            P(("seq", "head"), None, None),
            P(),
            P(),
        ),
        out_specs=P(("seq", "head"), None, None),
        check_vma=False,
    )
```

```python
from functools import partial

import jax
import jax.numpy as jnp
from jax import lax
from jax.experimental import pallas as pl
from jax.experimental.pallas import tpu as pltpu
from jax.sharding import PartitionSpec as P

BLK = 128


NEG_FILL = -1e30


def attend_kernel(slot_ref, which_ref, count_ref, query_ref, own_ref, mine0_ref, mine1_ref,
                  peer0_ref, peer1_ref, out_ref, block_buf, *, score_scale, slot_total, heads):
    row = pl.program_id(0)
    head_dim = block_buf.shape[2] // 2
    query = query_ref[...]
    query = jnp.concatenate(
        [query[:, h * head_dim:(h + 1) * head_dim] for h in range(heads)], axis=0
    )
    row_count = count_ref[row]
    sources = (mine0_ref, mine1_ref, peer0_ref, peer1_ref)
    for slot in range(1, slot_total):
        index = slot_ref[row, slot]
        which = which_ref[row, slot]
        for code, source in enumerate(sources):
            @pl.when(which == code)
            def _(source=source, slot=slot, index=index):
                block_buf[slot - 1] = source[index]
    scores = []
    values = []
    for slot in range(slot_total):
        block = own_ref[row] if slot == 0 else block_buf[slot - 1]
        key = block[:, :head_dim]
        value = block[:, head_dim:]
        part = lax.dot_general(
            query, key, (((1,), (1,)), ((), ())), preferred_element_type=jnp.float32
        ) * score_scale
        if slot > 0:
            part = jnp.where(slot < row_count, part, NEG_FILL)
        scores.append(part)
        values.append(value)
    row_max = jnp.max(scores[0], axis=1, keepdims=True)
    for part in scores[1:]:
        row_max = jnp.maximum(row_max, jnp.max(part, axis=1, keepdims=True))
    weights = [jnp.exp(part - row_max) for part in scores]
    total = jnp.sum(weights[0], axis=1, keepdims=True)
    for part in weights[1:]:
        total = total + jnp.sum(part, axis=1, keepdims=True)
    inverse = 1.0 / total
    acc = None
    for part, value in zip(weights, values):
        probs = (part * inverse).astype(jnp.bfloat16)
        term = jnp.dot(probs, value, preferred_element_type=jnp.float32)
        acc = term if acc is None else acc + term
    tokens = query_ref.shape[0]
    for h in range(heads):
        out_ref[:, h * head_dim:(h + 1) * head_dim] = acc[h * tokens:(h + 1) * tokens].astype(
            out_ref.dtype
        )


def attend_all(local_queries, column, width, own_blocks, received, slot_index, slot_which,
               row_counts, score_scale):
    seq_rows = local_queries.shape[0]
    qblocks, _, pair_dim = own_blocks.shape
    head_dim = pair_dim // 2
    slot_total = slot_index.shape[1]
    kernel = partial(
        attend_kernel, score_scale=score_scale, slot_total=slot_total, heads=width // head_dim
    )
    whole = lambda shape: pl.BlockSpec(shape, lambda r, s, w, c: (0,) * len(shape))
    return pl.pallas_call(
        kernel,
        out_shape=jax.ShapeDtypeStruct((seq_rows, width), local_queries.dtype),
        grid_spec=pltpu.PrefetchScalarGridSpec(
            num_scalar_prefetch=3,
            grid=(qblocks,),
            in_specs=[
                pl.BlockSpec((BLK, width), lambda r, s, w, c: (r, column)),
                whole(own_blocks.shape),
            ]
            + [whole(part.shape) for part in received],
            out_specs=pl.BlockSpec((BLK, width), lambda r, s, w, c: (r, 0)),
            scratch_shapes=[pltpu.VMEM((slot_total - 1, BLK, pair_dim), own_blocks.dtype)],
        ),
        compiler_params=pltpu.CompilerParams(vmem_limit_bytes=100 * 1024 * 1024),
    )(slot_index, slot_which, row_counts, local_queries, own_blocks, *received)


def make_plan(block_lists, block_counts, group_head, seq_index, shard_count, qblocks, capacity):
    slot_total = block_lists.shape[2]
    entries = qblocks * (slot_total - 1)
    row_lists = lax.dynamic_index_in_dim(block_lists, group_head, 0, keepdims=False)
    row_counts = lax.dynamic_index_in_dim(block_counts, group_head, 0, keepdims=False)
    slot_number = jnp.arange(1, slot_total, dtype=jnp.int32)
    live = (slot_number[None, :] < row_counts[:, None]).reshape(shard_count, entries)
    remote = row_lists[:, 1:].reshape(shard_count, entries)
    owner_shard = remote // qblocks
    within = remote % qblocks
    shard_ids = jnp.arange(shard_count, dtype=jnp.int32)
    hits = ((owner_shard[:, :, None] == shard_ids[None, None, :]) & live[:, :, None]).astype(
        jnp.int32
    )
    place = jnp.sum((jnp.cumsum(hits, axis=1) - hits) * hits, axis=2)
    mine = (live & (owner_shard == seq_index)).astype(jnp.int32)
    slot_match = (place[:, :, None] == jnp.arange(capacity, dtype=jnp.int32)[None, None, :]).astype(
        jnp.int32
    )
    chosen = jnp.sum(mine[:, :, None] * slot_match * within[:, :, None], axis=1)
    my_live = lax.dynamic_index_in_dim(live, seq_index, 0, keepdims=False)
    my_owner = lax.dynamic_index_in_dim(owner_shard, seq_index, 0, keepdims=False)
    my_place = jnp.minimum(lax.dynamic_index_in_dim(place, seq_index, 0, keepdims=False),
                           capacity - 1)
    my_counts = lax.dynamic_slice_in_dim(row_counts, seq_index * qblocks, qblocks, 0)
    return (chosen, my_live, my_owner, my_place, my_counts)


def on_device(queries, keys, values, block_lists, block_counts):
    head_count = lax.axis_size("head")
    shard_count = lax.axis_size("seq")
    head_index = lax.axis_index("head")
    seq_index = lax.axis_index("seq")
    tokens, query_heads, head_dim = queries.shape
    kv_total = keys.shape[1]
    assert head_count == 16 and kv_total == 8
    group_head = (head_index // 8) * 4 + head_index % 4
    half = (head_index // 4) % 2
    seq_rows = tokens * head_count
    qblocks = seq_rows // BLK
    group_size = query_heads // head_count
    slot_total = block_lists.shape[2]
    capacity = (qblocks * (slot_total - 1) + shard_count - 2) // (shard_count - 1)
    assert capacity == 4
    kv = jnp.concatenate([keys, values], axis=2)
    kv = jnp.transpose(kv.reshape(tokens, 2, 1, 4, 2 * head_dim), (1, 2, 3, 0, 4))
    kv = jnp.broadcast_to(kv, (2, 2, 4, tokens, 2 * head_dim))
    kv = kv.reshape(head_count, tokens, 2 * head_dim)
    own_blocks = lax.all_to_all(kv, "head", split_axis=0, concat_axis=0, tiled=True)
    chosen, my_live, my_owner, my_place, my_counts = make_plan(
        block_lists, block_counts, group_head, seq_index, shard_count, qblocks, capacity
    )
    partner = [(h, h ^ 4) for h in range(head_count)]
    mine = []
    peer = []
    for chunk in range(2):
        pick = lax.dynamic_index_in_dim(chosen, 2 * half + chunk, 1, keepdims=False)
        picked = own_blocks[pick]
        if chunk == 1:
            picked, _ = lax.optimization_barrier((picked, mine[0]))
        got = lax.all_to_all(picked, "seq", split_axis=0, concat_axis=0, tiled=True)
        mine.append(got)
        peer.append(lax.ppermute(got, "head", partner))
    spread = jnp.transpose(
        queries.reshape(tokens, 2, 4, 2, group_size, head_dim), (1, 3, 2, 0, 4, 5)
    ).reshape(head_count, tokens, group_size * head_dim)
    spread, _, _ = lax.optimization_barrier((spread, mine[1], peer[0]))
    local_queries = lax.all_to_all(spread, "head", split_axis=0, concat_axis=0, tiled=True)
    local_queries = local_queries.reshape(seq_rows, group_size * head_dim)
    which = jnp.where(my_place // 2 == half, 0, 2) + my_place % 2
    slot_index = jnp.where(my_live, my_owner, 0).reshape(qblocks, slot_total - 1)
    slot_which = jnp.where(my_live, which, 0).reshape(qblocks, slot_total - 1)
    zero_col = jnp.zeros((qblocks, 1), jnp.int32)
    slot_index = jnp.concatenate([zero_col, slot_index], axis=1)
    slot_which = jnp.concatenate([zero_col, slot_which], axis=1)
    score_scale = head_dim ** (-0.5)
    width = group_size * head_dim
    attended = attend_all(
        local_queries, 0, width, own_blocks, mine + peer, slot_index, slot_which,
        my_counts, score_scale
    )
    back = lax.all_to_all(
        attended.reshape(head_count, tokens, width), "head", split_axis=0, concat_axis=0,
        tiled=True
    )
    back = jnp.transpose(back.reshape(2, 2, 4, tokens, group_size, head_dim), (3, 0, 2, 1, 4, 5))
    return back.reshape(tokens, query_heads, head_dim)


def solution(mesh):
    return jax.shard_map(
        on_device,
        mesh=mesh,
        in_specs=(
            P(("seq", "head"), None, None),
            P(("seq", "head"), None, None),
            P(("seq", "head"), None, None),
            P(),
            P(),
        ),
        out_specs=P(("seq", "head"), None, None),
        check_vma=False,
    )
```

```python
from functools import partial

import jax
import jax.numpy as jnp
from jax import lax
from jax.experimental import pallas as pl
from jax.experimental.pallas import tpu as pltpu
from jax.sharding import PartitionSpec as P

BLK = 128


NEG_FILL = -1e30


def attend_kernel(slot_ref, which_ref, count_ref, query_ref, own_ref, mine0_ref, mine1_ref,
                  peer0_ref, peer1_ref, out_ref, block_buf, *, score_scale, slot_total, heads):
    row = pl.program_id(0)
    head_dim = block_buf.shape[2] // 2
    query = query_ref[...]
    query = jnp.concatenate(
        [query[:, h * head_dim:(h + 1) * head_dim] for h in range(heads)], axis=0
    )
    row_count = count_ref[row]
    sources = (mine0_ref, mine1_ref, peer0_ref, peer1_ref)
    for slot in range(1, slot_total):
        index = slot_ref[row, slot]
        which = which_ref[row, slot]
        for code, source in enumerate(sources):
            @pl.when(which == code)
            def _(source=source, slot=slot, index=index):
                block_buf[slot - 1] = source[index]
    scores = []
    values = []
    for slot in range(slot_total):
        block = own_ref[row] if slot == 0 else block_buf[slot - 1]
        key = block[:, :head_dim]
        value = block[:, head_dim:]
        part = lax.dot_general(
            query, key, (((1,), (1,)), ((), ())), preferred_element_type=jnp.float32
        ) * score_scale
        if slot > 0:
            part = jnp.where(slot < row_count, part, NEG_FILL)
        scores.append(part)
        values.append(value)
    lane_max = scores[0]
    for part in scores[1:]:
        lane_max = jnp.maximum(lane_max, part)
    row_max = jnp.max(lane_max, axis=1, keepdims=True)
    weights = [jnp.exp(part - row_max) for part in scores]
    lane_sum = weights[0]
    for part in weights[1:]:
        lane_sum = lane_sum + part
    inverse = 1.0 / jnp.sum(lane_sum, axis=1, keepdims=True)
    acc = None
    for part, value in zip(weights, values):
        probs = (part * inverse).astype(jnp.bfloat16)
        term = jnp.dot(probs, value, preferred_element_type=jnp.float32)
        acc = term if acc is None else acc + term
    tokens = query_ref.shape[0]
    for h in range(heads):
        out_ref[:, h * head_dim:(h + 1) * head_dim] = acc[h * tokens:(h + 1) * tokens].astype(
            out_ref.dtype
        )


def attend_all(local_queries, column, width, own_blocks, received, slot_index, slot_which,
               row_counts, score_scale):
    seq_rows = local_queries.shape[0]
    qblocks, _, pair_dim = own_blocks.shape
    head_dim = pair_dim // 2
    slot_total = slot_index.shape[1]
    kernel = partial(
        attend_kernel, score_scale=score_scale, slot_total=slot_total, heads=width // head_dim
    )
    whole = lambda shape: pl.BlockSpec(shape, lambda r, s, w, c: (0,) * len(shape))
    return pl.pallas_call(
        kernel,
        out_shape=jax.ShapeDtypeStruct((seq_rows, width), local_queries.dtype),
        grid_spec=pltpu.PrefetchScalarGridSpec(
            num_scalar_prefetch=3,
            grid=(qblocks,),
            in_specs=[
                pl.BlockSpec((BLK, width), lambda r, s, w, c: (r, column)),
                whole(own_blocks.shape),
            ]
            + [whole(part.shape) for part in received],
            out_specs=pl.BlockSpec((BLK, width), lambda r, s, w, c: (r, 0)),
            scratch_shapes=[pltpu.VMEM((slot_total - 1, BLK, pair_dim), own_blocks.dtype)],
        ),
        compiler_params=pltpu.CompilerParams(vmem_limit_bytes=100 * 1024 * 1024),
    )(slot_index, slot_which, row_counts, local_queries, own_blocks, *received)


def make_plan(block_lists, block_counts, group_head, seq_index, shard_count, qblocks, capacity):
    slot_total = block_lists.shape[2]
    entries = qblocks * (slot_total - 1)
    row_lists = lax.dynamic_index_in_dim(block_lists, group_head, 0, keepdims=False)
    row_counts = lax.dynamic_index_in_dim(block_counts, group_head, 0, keepdims=False)
    slot_number = jnp.arange(1, slot_total, dtype=jnp.int32)
    live = (slot_number[None, :] < row_counts[:, None]).reshape(shard_count, entries)
    remote = row_lists[:, 1:].reshape(shard_count, entries)
    owner_shard = remote // qblocks
    within = remote % qblocks
    shard_ids = jnp.arange(shard_count, dtype=jnp.int32)
    hits = ((owner_shard[:, :, None] == shard_ids[None, None, :]) & live[:, :, None]).astype(
        jnp.int32
    )
    place = jnp.sum((jnp.cumsum(hits, axis=1) - hits) * hits, axis=2)
    mine = (live & (owner_shard == seq_index)).astype(jnp.int32)
    slot_match = (place[:, :, None] == jnp.arange(capacity, dtype=jnp.int32)[None, None, :]).astype(
        jnp.int32
    )
    chosen = jnp.sum(mine[:, :, None] * slot_match * within[:, :, None], axis=1)
    my_live = lax.dynamic_index_in_dim(live, seq_index, 0, keepdims=False)
    my_owner = lax.dynamic_index_in_dim(owner_shard, seq_index, 0, keepdims=False)
    my_place = jnp.minimum(lax.dynamic_index_in_dim(place, seq_index, 0, keepdims=False),
                           capacity - 1)
    my_counts = lax.dynamic_slice_in_dim(row_counts, seq_index * qblocks, qblocks, 0)
    return (chosen, my_live, my_owner, my_place, my_counts)


def on_device(queries, keys, values, block_lists, block_counts):
    head_count = lax.axis_size("head")
    shard_count = lax.axis_size("seq")
    head_index = lax.axis_index("head")
    seq_index = lax.axis_index("seq")
    tokens, query_heads, head_dim = queries.shape
    kv_total = keys.shape[1]
    assert head_count == 16 and kv_total == 8
    group_head = (head_index // 8) * 4 + head_index % 4
    half = (head_index // 4) % 2
    seq_rows = tokens * head_count
    qblocks = seq_rows // BLK
    group_size = query_heads // head_count
    slot_total = block_lists.shape[2]
    capacity = (qblocks * (slot_total - 1) + shard_count - 2) // (shard_count - 1)
    assert capacity == 4
    kv = jnp.concatenate([keys, values], axis=2)
    kv = jnp.transpose(kv.reshape(tokens, 2, 1, 4, 2 * head_dim), (1, 2, 3, 0, 4))
    kv = jnp.broadcast_to(kv, (2, 2, 4, tokens, 2 * head_dim))
    kv = kv.reshape(head_count, tokens, 2 * head_dim)
    own_blocks = lax.all_to_all(kv, "head", split_axis=0, concat_axis=0, tiled=True)
    chosen, my_live, my_owner, my_place, my_counts = make_plan(
        block_lists, block_counts, group_head, seq_index, shard_count, qblocks, capacity
    )
    partner = [(h, h ^ 4) for h in range(head_count)]
    mine = []
    peer = []
    for chunk in range(2):
        pick = lax.dynamic_index_in_dim(chosen, 2 * half + chunk, 1, keepdims=False)
        picked = own_blocks[pick]
        if chunk == 1:
            picked, _ = lax.optimization_barrier((picked, mine[0]))
        got = lax.all_to_all(picked, "seq", split_axis=0, concat_axis=0, tiled=True)
        mine.append(got)
        peer.append(lax.ppermute(got, "head", partner))
    spread = jnp.transpose(
        queries.reshape(tokens, 2, 4, 2, group_size, head_dim), (1, 3, 2, 0, 4, 5)
    ).reshape(head_count, tokens, group_size * head_dim)
    spread, _, _ = lax.optimization_barrier((spread, mine[1], peer[0]))
    local_queries = lax.all_to_all(spread, "head", split_axis=0, concat_axis=0, tiled=True)
    local_queries = local_queries.reshape(seq_rows, group_size * head_dim)
    which = jnp.where(my_place // 2 == half, 0, 2) + my_place % 2
    slot_index = jnp.where(my_live, my_owner, 0).reshape(qblocks, slot_total - 1)
    slot_which = jnp.where(my_live, which, 0).reshape(qblocks, slot_total - 1)
    zero_col = jnp.zeros((qblocks, 1), jnp.int32)
    slot_index = jnp.concatenate([zero_col, slot_index], axis=1)
    slot_which = jnp.concatenate([zero_col, slot_which], axis=1)
    score_scale = head_dim ** (-0.5)
    width = group_size * head_dim
    attended = attend_all(
        local_queries, 0, width, own_blocks, mine + peer, slot_index, slot_which,
        my_counts, score_scale
    )
    back = lax.all_to_all(
        attended.reshape(head_count, tokens, width), "head", split_axis=0, concat_axis=0,
        tiled=True
    )
    back = jnp.transpose(back.reshape(2, 2, 4, tokens, group_size, head_dim), (3, 0, 2, 1, 4, 5))
    return back.reshape(tokens, query_heads, head_dim)


def solution(mesh):
    return jax.shard_map(
        on_device,
        mesh=mesh,
        in_specs=(
            P(("seq", "head"), None, None),
            P(("seq", "head"), None, None),
            P(("seq", "head"), None, None),
            P(),
            P(),
        ),
        out_specs=P(("seq", "head"), None, None),
        check_vma=False,
    )
```

```python
from functools import partial

import jax
import jax.numpy as jnp
from jax import lax
from jax.experimental import pallas as pl
from jax.experimental.pallas import tpu as pltpu
from jax.sharding import PartitionSpec as P

BLK = 128


NEG_FILL = -1e30


def attend_kernel(slot_ref, which_ref, count_ref, qrow_ref, query_ref, own_ref, mine0_ref, mine1_ref,
                  peer0_ref, peer1_ref, out_ref, block_buf, *, score_scale, slot_total, heads):
    row = pl.program_id(0)
    head_dim = block_buf.shape[2] // 2
    query = query_ref[...]
    query = jnp.concatenate(
        [query[:, h * head_dim:(h + 1) * head_dim] for h in range(heads)], axis=0
    )
    row_count = count_ref[row]
    sources = (mine0_ref, mine1_ref, peer0_ref, peer1_ref)
    for slot in range(1, slot_total):
        index = slot_ref[row, slot]
        which = which_ref[row, slot]
        for code, source in enumerate(sources):
            @pl.when(which == code)
            def _(source=source, slot=slot, index=index):
                block_buf[slot - 1] = source[index]
    scores = []
    values = []
    for slot in range(slot_total):
        block = own_ref[row] if slot == 0 else block_buf[slot - 1]
        key = block[:, :head_dim]
        value = block[:, head_dim:]
        part = lax.dot_general(
            query, key, (((1,), (1,)), ((), ())), preferred_element_type=jnp.float32
        ) * score_scale
        if slot > 0:
            part = jnp.where(slot < row_count, part, NEG_FILL)
        scores.append(part)
        values.append(value)
    lane_max = scores[0]
    for part in scores[1:]:
        lane_max = jnp.maximum(lane_max, part)
    row_max = jnp.max(lane_max, axis=1, keepdims=True)
    weights = [jnp.exp(part - row_max) for part in scores]
    lane_sum = weights[0]
    for part in weights[1:]:
        lane_sum = lane_sum + part
    inverse = 1.0 / jnp.sum(lane_sum, axis=1, keepdims=True)
    acc = None
    for part, value in zip(weights, values):
        probs = (part * inverse).astype(jnp.bfloat16)
        term = jnp.dot(probs, value, preferred_element_type=jnp.float32)
        acc = term if acc is None else acc + term
    tokens = query_ref.shape[0]
    for h in range(heads):
        out_ref[:, h * head_dim:(h + 1) * head_dim] = acc[h * tokens:(h + 1) * tokens].astype(
            out_ref.dtype
        )


def attend_all(local_queries, query_row, width, own_blocks, received, slot_index, slot_which,
               row_counts, score_scale):
    seq_rows = local_queries.shape[0] * local_queries.shape[1]
    qblocks, _, pair_dim = own_blocks.shape
    head_dim = pair_dim // 2
    slot_total = slot_index.shape[1]
    kernel = partial(
        attend_kernel, score_scale=score_scale, slot_total=slot_total, heads=width // head_dim
    )
    whole = lambda shape: pl.BlockSpec(shape, lambda r, s, w, c, q: (0,) * len(shape))
    return pl.pallas_call(
        kernel,
        out_shape=jax.ShapeDtypeStruct((seq_rows, width), local_queries.dtype),
        grid_spec=pltpu.PrefetchScalarGridSpec(
            num_scalar_prefetch=4,
            grid=(qblocks,),
            in_specs=[
                pl.BlockSpec((None, BLK, width), lambda r, s, w, c, q: (q[r], 0, 0)),
                whole(own_blocks.shape),
            ]
            + [whole(part.shape) for part in received],
            out_specs=pl.BlockSpec((BLK, width), lambda r, s, w, c, q: (r, 0)),
            scratch_shapes=[pltpu.VMEM((slot_total - 1, BLK, pair_dim), own_blocks.dtype)],
        ),
        compiler_params=pltpu.CompilerParams(vmem_limit_bytes=100 * 1024 * 1024),
    )(slot_index, slot_which, row_counts, query_row, local_queries, own_blocks, *received)


def make_plan(block_lists, block_counts, group_head, seq_index, shard_count, qblocks, capacity):
    slot_total = block_lists.shape[2]
    entries = qblocks * (slot_total - 1)
    row_lists = lax.dynamic_index_in_dim(block_lists, group_head, 0, keepdims=False)
    row_counts = lax.dynamic_index_in_dim(block_counts, group_head, 0, keepdims=False)
    slot_number = jnp.arange(1, slot_total, dtype=jnp.int32)
    live = (slot_number[None, :] < row_counts[:, None]).reshape(shard_count, entries)
    remote = row_lists[:, 1:].reshape(shard_count, entries)
    owner_shard = remote // qblocks
    within = remote % qblocks
    shard_ids = jnp.arange(shard_count, dtype=jnp.int32)
    hits = ((owner_shard[:, :, None] == shard_ids[None, None, :]) & live[:, :, None]).astype(
        jnp.int32
    )
    place = jnp.sum((jnp.cumsum(hits, axis=1) - hits) * hits, axis=2)
    mine = (live & (owner_shard == seq_index)).astype(jnp.int32)
    slot_match = (place[:, :, None] == jnp.arange(capacity, dtype=jnp.int32)[None, None, :]).astype(
        jnp.int32
    )
    chosen = jnp.sum(mine[:, :, None] * slot_match * within[:, :, None], axis=1)
    my_live = lax.dynamic_index_in_dim(live, seq_index, 0, keepdims=False)
    my_owner = lax.dynamic_index_in_dim(owner_shard, seq_index, 0, keepdims=False)
    my_place = jnp.minimum(lax.dynamic_index_in_dim(place, seq_index, 0, keepdims=False),
                           capacity - 1)
    my_counts = lax.dynamic_slice_in_dim(row_counts, seq_index * qblocks, qblocks, 0)
    return (chosen, my_live, my_owner, my_place, my_counts)


def on_device(queries, keys, values, block_lists, block_counts):
    head_count = lax.axis_size("head")
    shard_count = lax.axis_size("seq")
    head_index = lax.axis_index("head")
    seq_index = lax.axis_index("seq")
    tokens, query_heads, head_dim = queries.shape
    kv_total = keys.shape[1]
    assert head_count == 16 and kv_total == 8
    group_head = (head_index // 8) * 4 + head_index % 4
    half = (head_index // 4) % 2
    seq_rows = tokens * head_count
    qblocks = seq_rows // BLK
    group_size = query_heads // head_count
    slot_total = block_lists.shape[2]
    capacity = (qblocks * (slot_total - 1) + shard_count - 2) // (shard_count - 1)
    assert capacity == 4
    kv = jnp.concatenate([keys, values], axis=2)
    kv = jnp.transpose(kv.reshape(tokens, 2, 1, 4, 2 * head_dim), (1, 2, 3, 0, 4))
    kv = jnp.broadcast_to(kv, (2, 2, 4, tokens, 2 * head_dim))
    kv = kv.reshape(head_count, tokens, 2 * head_dim)
    own_blocks = lax.all_to_all(kv, "head", split_axis=0, concat_axis=0, tiled=True)
    chosen, my_live, my_owner, my_place, my_counts = make_plan(
        block_lists, block_counts, group_head, seq_index, shard_count, qblocks, capacity
    )
    partner = [(h, h ^ 4) for h in range(head_count)]
    mine = []
    peer = []
    for chunk in range(2):
        pick = lax.dynamic_index_in_dim(chosen, 2 * half + chunk, 1, keepdims=False)
        picked = own_blocks[pick]
        if chunk == 1:
            picked, _ = lax.optimization_barrier((picked, mine[0]))
        got = lax.all_to_all(picked, "seq", split_axis=0, concat_axis=0, tiled=True)
        mine.append(got)
        peer.append(lax.ppermute(got, "head", partner))
    spread = jnp.transpose(
        queries.reshape(tokens, 2, 4, 2, group_size, head_dim), (1, 3, 2, 0, 4, 5)
    ).reshape(head_count, tokens, group_size * head_dim)
    pieces = [lax.dynamic_index_in_dim(spread, head_index, 0, keepdims=False)]
    for shift in range(1, head_count):
        piece = lax.dynamic_index_in_dim(spread, (head_index + shift) % head_count, 0,
                                         keepdims=False)
        pieces.append(lax.ppermute(
            piece, "head", [(h, (h + shift) % head_count) for h in range(head_count)]
        ))
    local_queries = jnp.stack(pieces)
    query_row = (head_index - jnp.arange(qblocks, dtype=jnp.int32)) % head_count
    which = jnp.where(my_place // 2 == half, 0, 2) + my_place % 2
    slot_index = jnp.where(my_live, my_owner, 0).reshape(qblocks, slot_total - 1)
    slot_which = jnp.where(my_live, which, 0).reshape(qblocks, slot_total - 1)
    zero_col = jnp.zeros((qblocks, 1), jnp.int32)
    slot_index = jnp.concatenate([zero_col, slot_index], axis=1)
    slot_which = jnp.concatenate([zero_col, slot_which], axis=1)
    score_scale = head_dim ** (-0.5)
    width = group_size * head_dim
    attended = attend_all(
        local_queries, query_row, width, own_blocks, mine + peer, slot_index, slot_which,
        my_counts, score_scale
    )
    back = lax.all_to_all(
        attended.reshape(head_count, tokens, width), "head", split_axis=0, concat_axis=0,
        tiled=True
    )
    back = jnp.transpose(back.reshape(2, 2, 4, tokens, group_size, head_dim), (3, 0, 2, 1, 4, 5))
    return back.reshape(tokens, query_heads, head_dim)


def solution(mesh):
    return jax.shard_map(
        on_device,
        mesh=mesh,
        in_specs=(
            P(("seq", "head"), None, None),
            P(("seq", "head"), None, None),
            P(("seq", "head"), None, None),
            P(),
            P(),
        ),
        out_specs=P(("seq", "head"), None, None),
        check_vma=False,
    )
```

```python
from functools import partial

import jax
import jax.numpy as jnp
from jax import lax
from jax.experimental import pallas as pl
from jax.experimental.pallas import tpu as pltpu
from jax.sharding import PartitionSpec as P

BLK = 128


NEG_FILL = -1e30


def attend_kernel(slot_ref, which_ref, count_ref, query_ref, own_ref, mine0_ref, mine1_ref,
                  peer0_ref, peer1_ref, out_ref, block_buf, *, score_scale, slot_total, heads):
    row = pl.program_id(0)
    head_dim = block_buf.shape[1] // 2
    query = query_ref[...]
    query = jnp.concatenate(
        [query[:, h * head_dim:(h + 1) * head_dim] for h in range(heads)], axis=0
    )
    row_count = count_ref[row]
    sources = (mine0_ref, mine1_ref, peer0_ref, peer1_ref)
    block_buf[0:BLK] = own_ref[row]
    for slot in range(1, slot_total):
        index = slot_ref[row, slot]
        which = which_ref[row, slot]
        for code, source in enumerate(sources):
            @pl.when(which == code)
            def _(source=source, slot=slot, index=index):
                block_buf[slot * BLK:(slot + 1) * BLK] = source[index]
    blocks = block_buf[...]
    keys = blocks[:, :head_dim]
    values = blocks[:, head_dim:]
    scores = lax.dot_general(
        query, keys, (((1,), (1,)), ((), ())), preferred_element_type=jnp.float32
    ) * score_scale
    key_slot = lax.broadcasted_iota(jnp.int32, (1, slot_total * BLK), 1) // BLK
    scores = jnp.where(key_slot < row_count, scores, NEG_FILL)
    row_max = jnp.max(scores, axis=1, keepdims=True)
    weights = jnp.exp(scores - row_max)
    inverse = 1.0 / jnp.sum(weights, axis=1, keepdims=True)
    probs = (weights * inverse).astype(jnp.bfloat16)
    acc = jnp.dot(probs, values, preferred_element_type=jnp.float32)
    tokens = query_ref.shape[0]
    for h in range(heads):
        out_ref[:, h * head_dim:(h + 1) * head_dim] = acc[h * tokens:(h + 1) * tokens].astype(
            out_ref.dtype
        )


def attend_all(local_queries, column, width, own_blocks, received, slot_index, slot_which,
               row_counts, score_scale):
    seq_rows = local_queries.shape[0]
    qblocks, _, pair_dim = own_blocks.shape
    head_dim = pair_dim // 2
    slot_total = slot_index.shape[1]
    kernel = partial(
        attend_kernel, score_scale=score_scale, slot_total=slot_total, heads=width // head_dim
    )
    whole = lambda shape: pl.BlockSpec(shape, lambda r, s, w, c: (0,) * len(shape))
    return pl.pallas_call(
        kernel,
        out_shape=jax.ShapeDtypeStruct((seq_rows, width), local_queries.dtype),
        grid_spec=pltpu.PrefetchScalarGridSpec(
            num_scalar_prefetch=3,
            grid=(qblocks,),
            in_specs=[
                pl.BlockSpec((BLK, width), lambda r, s, w, c: (r, column)),
                whole(own_blocks.shape),
            ]
            + [whole(part.shape) for part in received],
            out_specs=pl.BlockSpec((BLK, width), lambda r, s, w, c: (r, 0)),
            scratch_shapes=[pltpu.VMEM((slot_total * BLK, pair_dim), own_blocks.dtype)],
        ),
        compiler_params=pltpu.CompilerParams(vmem_limit_bytes=100 * 1024 * 1024),
    )(slot_index, slot_which, row_counts, local_queries, own_blocks, *received)


def make_plan(block_lists, block_counts, group_head, seq_index, shard_count, qblocks, capacity):
    slot_total = block_lists.shape[2]
    entries = qblocks * (slot_total - 1)
    row_lists = lax.dynamic_index_in_dim(block_lists, group_head, 0, keepdims=False)
    row_counts = lax.dynamic_index_in_dim(block_counts, group_head, 0, keepdims=False)
    slot_number = jnp.arange(1, slot_total, dtype=jnp.int32)
    live = (slot_number[None, :] < row_counts[:, None]).reshape(shard_count, entries)
    remote = row_lists[:, 1:].reshape(shard_count, entries)
    owner_shard = remote // qblocks
    within = remote % qblocks
    shard_ids = jnp.arange(shard_count, dtype=jnp.int32)
    hits = ((owner_shard[:, :, None] == shard_ids[None, None, :]) & live[:, :, None]).astype(
        jnp.int32
    )
    place = jnp.sum((jnp.cumsum(hits, axis=1) - hits) * hits, axis=2)
    mine = (live & (owner_shard == seq_index)).astype(jnp.int32)
    slot_match = (place[:, :, None] == jnp.arange(capacity, dtype=jnp.int32)[None, None, :]).astype(
        jnp.int32
    )
    chosen = jnp.sum(mine[:, :, None] * slot_match * within[:, :, None], axis=1)
    my_live = lax.dynamic_index_in_dim(live, seq_index, 0, keepdims=False)
    my_owner = lax.dynamic_index_in_dim(owner_shard, seq_index, 0, keepdims=False)
    my_place = jnp.minimum(lax.dynamic_index_in_dim(place, seq_index, 0, keepdims=False),
                           capacity - 1)
    my_counts = lax.dynamic_slice_in_dim(row_counts, seq_index * qblocks, qblocks, 0)
    return (chosen, my_live, my_owner, my_place, my_counts)


def on_device(queries, keys, values, block_lists, block_counts):
    head_count = lax.axis_size("head")
    shard_count = lax.axis_size("seq")
    head_index = lax.axis_index("head")
    seq_index = lax.axis_index("seq")
    tokens, query_heads, head_dim = queries.shape
    kv_total = keys.shape[1]
    assert head_count == 16 and kv_total == 8
    group_head = (head_index // 8) * 4 + head_index % 4
    half = (head_index // 4) % 2
    seq_rows = tokens * head_count
    qblocks = seq_rows // BLK
    group_size = query_heads // head_count
    slot_total = block_lists.shape[2]
    capacity = (qblocks * (slot_total - 1) + shard_count - 2) // (shard_count - 1)
    assert capacity == 4
    kv = jnp.concatenate([keys, values], axis=2)
    kv = jnp.transpose(kv.reshape(tokens, 2, 1, 4, 2 * head_dim), (1, 2, 3, 0, 4))
    kv = jnp.broadcast_to(kv, (2, 2, 4, tokens, 2 * head_dim))
    kv = kv.reshape(head_count, tokens, 2 * head_dim)
    own_blocks = lax.all_to_all(kv, "head", split_axis=0, concat_axis=0, tiled=True)
    chosen, my_live, my_owner, my_place, my_counts = make_plan(
        block_lists, block_counts, group_head, seq_index, shard_count, qblocks, capacity
    )
    partner = [(h, h ^ 4) for h in range(head_count)]
    mine = []
    peer = []
    for chunk in range(2):
        pick = lax.dynamic_index_in_dim(chosen, 2 * half + chunk, 1, keepdims=False)
        picked = own_blocks[pick]
        if chunk == 1:
            picked, _ = lax.optimization_barrier((picked, mine[0]))
        got = lax.all_to_all(picked, "seq", split_axis=0, concat_axis=0, tiled=True)
        mine.append(got)
        peer.append(lax.ppermute(got, "head", partner))
    spread = jnp.transpose(
        queries.reshape(tokens, 2, 4, 2, group_size, head_dim), (1, 3, 2, 0, 4, 5)
    ).reshape(head_count, tokens, group_size * head_dim)
    spread, _, _ = lax.optimization_barrier((spread, mine[1], peer[0]))
    local_queries = lax.all_to_all(spread, "head", split_axis=0, concat_axis=0, tiled=True)
    local_queries = local_queries.reshape(seq_rows, group_size * head_dim)
    which = jnp.where(my_place // 2 == half, 0, 2) + my_place % 2
    slot_index = jnp.where(my_live, my_owner, 0).reshape(qblocks, slot_total - 1)
    slot_which = jnp.where(my_live, which, 0).reshape(qblocks, slot_total - 1)
    zero_col = jnp.zeros((qblocks, 1), jnp.int32)
    slot_index = jnp.concatenate([zero_col, slot_index], axis=1)
    slot_which = jnp.concatenate([zero_col, slot_which], axis=1)
    score_scale = head_dim ** (-0.5)
    width = group_size * head_dim
    attended = attend_all(
        local_queries, 0, width, own_blocks, mine + peer, slot_index, slot_which,
        my_counts, score_scale
    )
    back = lax.all_to_all(
        attended.reshape(head_count, tokens, width), "head", split_axis=0, concat_axis=0,
        tiled=True
    )
    back = jnp.transpose(back.reshape(2, 2, 4, tokens, group_size, head_dim), (3, 0, 2, 1, 4, 5))
    return back.reshape(tokens, query_heads, head_dim)


def solution(mesh):
    return jax.shard_map(
        on_device,
        mesh=mesh,
        in_specs=(
            P(("seq", "head"), None, None),
            P(("seq", "head"), None, None),
            P(("seq", "head"), None, None),
            P(),
            P(),
        ),
        out_specs=P(("seq", "head"), None, None),
        check_vma=False,
    )
```

```python
from functools import partial

import jax
import jax.numpy as jnp
from jax import lax
from jax.experimental import pallas as pl
from jax.experimental.pallas import tpu as pltpu
from jax.sharding import PartitionSpec as P

BLK = 128


NEG_FILL = -1e30
LOG2_E = 1.4426950408889634


def attend_kernel(slot_ref, which_ref, count_ref, query_ref, own_ref, mine0_ref, mine1_ref,
                  peer0_ref, peer1_ref, out_ref, block_buf, *, score_scale, slot_total, heads):
    row = pl.program_id(0)
    head_dim = block_buf.shape[1] // 2
    query = query_ref[...]
    query = jnp.concatenate(
        [query[:, h * head_dim:(h + 1) * head_dim] for h in range(heads)], axis=0
    )
    row_count = count_ref[row]
    sources = (mine0_ref, mine1_ref, peer0_ref, peer1_ref)
    block_buf[0:BLK] = own_ref[row]
    for slot in range(1, slot_total):
        index = slot_ref[row, slot]
        which = which_ref[row, slot]
        for code, source in enumerate(sources):
            @pl.when(which == code)
            def _(source=source, slot=slot, index=index):
                block_buf[slot * BLK:(slot + 1) * BLK] = source[index]
    blocks = block_buf[...]
    keys = blocks[:, :head_dim]
    values = blocks[:, head_dim:]
    scores = lax.dot_general(
        query, keys, (((1,), (1,)), ((), ())), preferred_element_type=jnp.float32
    )
    key_slot = lax.broadcasted_iota(jnp.int32, (1, slot_total * BLK), 1) // BLK
    scores = jnp.where(key_slot < row_count, scores, NEG_FILL)
    row_max = jnp.max(scores, axis=1, keepdims=True)
    weights = jnp.exp2((scores - row_max) * (score_scale * LOG2_E))
    inverse = 1.0 / jnp.sum(weights, axis=1, keepdims=True)
    acc = jnp.dot(weights.astype(jnp.bfloat16), values, preferred_element_type=jnp.float32)
    acc = acc * inverse
    tokens = query_ref.shape[0]
    for h in range(heads):
        out_ref[:, h * head_dim:(h + 1) * head_dim] = acc[h * tokens:(h + 1) * tokens].astype(
            out_ref.dtype
        )


def attend_all(local_queries, column, width, own_blocks, received, slot_index, slot_which,
               row_counts, score_scale):
    seq_rows = local_queries.shape[0]
    qblocks, _, pair_dim = own_blocks.shape
    head_dim = pair_dim // 2
    slot_total = slot_index.shape[1]
    kernel = partial(
        attend_kernel, score_scale=score_scale, slot_total=slot_total, heads=width // head_dim
    )
    whole = lambda shape: pl.BlockSpec(shape, lambda r, s, w, c: (0,) * len(shape))
    return pl.pallas_call(
        kernel,
        out_shape=jax.ShapeDtypeStruct((seq_rows, width), local_queries.dtype),
        grid_spec=pltpu.PrefetchScalarGridSpec(
            num_scalar_prefetch=3,
            grid=(qblocks,),
            in_specs=[
                pl.BlockSpec((BLK, width), lambda r, s, w, c: (r, column)),
                whole(own_blocks.shape),
            ]
            + [whole(part.shape) for part in received],
            out_specs=pl.BlockSpec((BLK, width), lambda r, s, w, c: (r, 0)),
            scratch_shapes=[pltpu.VMEM((slot_total * BLK, pair_dim), own_blocks.dtype)],
        ),
        compiler_params=pltpu.CompilerParams(vmem_limit_bytes=100 * 1024 * 1024),
    )(slot_index, slot_which, row_counts, local_queries, own_blocks, *received)


def make_plan(block_lists, block_counts, group_head, seq_index, shard_count, qblocks, capacity):
    slot_total = block_lists.shape[2]
    entries = qblocks * (slot_total - 1)
    row_lists = lax.dynamic_index_in_dim(block_lists, group_head, 0, keepdims=False)
    row_counts = lax.dynamic_index_in_dim(block_counts, group_head, 0, keepdims=False)
    slot_number = jnp.arange(1, slot_total, dtype=jnp.int32)
    live = (slot_number[None, :] < row_counts[:, None]).reshape(shard_count, entries)
    remote = row_lists[:, 1:].reshape(shard_count, entries)
    owner_shard = remote // qblocks
    within = remote % qblocks
    shard_ids = jnp.arange(shard_count, dtype=jnp.int32)
    hits = ((owner_shard[:, :, None] == shard_ids[None, None, :]) & live[:, :, None]).astype(
        jnp.int32
    )
    place = jnp.sum((jnp.cumsum(hits, axis=1) - hits) * hits, axis=2)
    mine = (live & (owner_shard == seq_index)).astype(jnp.int32)
    slot_match = (place[:, :, None] == jnp.arange(capacity, dtype=jnp.int32)[None, None, :]).astype(
        jnp.int32
    )
    chosen = jnp.sum(mine[:, :, None] * slot_match * within[:, :, None], axis=1)
    my_live = lax.dynamic_index_in_dim(live, seq_index, 0, keepdims=False)
    my_owner = lax.dynamic_index_in_dim(owner_shard, seq_index, 0, keepdims=False)
    my_place = jnp.minimum(lax.dynamic_index_in_dim(place, seq_index, 0, keepdims=False),
                           capacity - 1)
    my_counts = lax.dynamic_slice_in_dim(row_counts, seq_index * qblocks, qblocks, 0)
    return (chosen, my_live, my_owner, my_place, my_counts)


def on_device(queries, keys, values, block_lists, block_counts):
    head_count = lax.axis_size("head")
    shard_count = lax.axis_size("seq")
    head_index = lax.axis_index("head")
    seq_index = lax.axis_index("seq")
    tokens, query_heads, head_dim = queries.shape
    kv_total = keys.shape[1]
    assert head_count == 16 and kv_total == 8
    group_head = (head_index // 8) * 4 + head_index % 4
    half = (head_index // 4) % 2
    seq_rows = tokens * head_count
    qblocks = seq_rows // BLK
    group_size = query_heads // head_count
    slot_total = block_lists.shape[2]
    capacity = (qblocks * (slot_total - 1) + shard_count - 2) // (shard_count - 1)
    assert capacity == 4
    kv = jnp.concatenate([keys, values], axis=2)
    kv = jnp.transpose(kv.reshape(tokens, 2, 1, 4, 2 * head_dim), (1, 2, 3, 0, 4))
    kv = jnp.broadcast_to(kv, (2, 2, 4, tokens, 2 * head_dim))
    kv = kv.reshape(head_count, tokens, 2 * head_dim)
    own_blocks = lax.all_to_all(kv, "head", split_axis=0, concat_axis=0, tiled=True)
    chosen, my_live, my_owner, my_place, my_counts = make_plan(
        block_lists, block_counts, group_head, seq_index, shard_count, qblocks, capacity
    )
    partner = [(h, h ^ 4) for h in range(head_count)]
    mine = []
    peer = []
    for chunk in range(2):
        pick = lax.dynamic_index_in_dim(chosen, 2 * half + chunk, 1, keepdims=False)
        picked = own_blocks[pick]
        if chunk == 1:
            picked, _ = lax.optimization_barrier((picked, mine[0]))
        got = lax.all_to_all(picked, "seq", split_axis=0, concat_axis=0, tiled=True)
        mine.append(got)
        peer.append(lax.ppermute(got, "head", partner))
    spread = jnp.transpose(
        queries.reshape(tokens, 2, 4, 2, group_size, head_dim), (1, 3, 2, 0, 4, 5)
    ).reshape(head_count, tokens, group_size * head_dim)
    spread, _, _ = lax.optimization_barrier((spread, mine[1], peer[0]))
    local_queries = lax.all_to_all(spread, "head", split_axis=0, concat_axis=0, tiled=True)
    local_queries = local_queries.reshape(seq_rows, group_size * head_dim)
    which = jnp.where(my_place // 2 == half, 0, 2) + my_place % 2
    slot_index = jnp.where(my_live, my_owner, 0).reshape(qblocks, slot_total - 1)
    slot_which = jnp.where(my_live, which, 0).reshape(qblocks, slot_total - 1)
    zero_col = jnp.zeros((qblocks, 1), jnp.int32)
    slot_index = jnp.concatenate([zero_col, slot_index], axis=1)
    slot_which = jnp.concatenate([zero_col, slot_which], axis=1)
    score_scale = head_dim ** (-0.5)
    width = group_size * head_dim
    attended = attend_all(
        local_queries, 0, width, own_blocks, mine + peer, slot_index, slot_which,
        my_counts, score_scale
    )
    back = lax.all_to_all(
        attended.reshape(head_count, tokens, width), "head", split_axis=0, concat_axis=0,
        tiled=True
    )
    back = jnp.transpose(back.reshape(2, 2, 4, tokens, group_size, head_dim), (3, 0, 2, 1, 4, 5))
    return back.reshape(tokens, query_heads, head_dim)


def solution(mesh):
    return jax.shard_map(
        on_device,
        mesh=mesh,
        in_specs=(
            P(("seq", "head"), None, None),
            P(("seq", "head"), None, None),
            P(("seq", "head"), None, None),
            P(),
            P(),
        ),
        out_specs=P(("seq", "head"), None, None),
        check_vma=False,
    )
```

```python
from functools import partial

import jax
import jax.numpy as jnp
from jax import lax
from jax.experimental import pallas as pl
from jax.experimental.pallas import tpu as pltpu
from jax.sharding import PartitionSpec as P

BLK = 128


NEG_FILL = -1e30
LOG2_E = 1.4426950408889634


def attend_kernel(slot_ref, which_ref, count_ref, query_ref, own_ref, mine0_ref, mine1_ref,
                  peer0_ref, peer1_ref, out_ref, block_buf, *, score_scale, slot_total, heads):
    row = pl.program_id(0)
    head_dim = block_buf.shape[1] // 2
    query = query_ref[...]
    query = jnp.concatenate(
        [query[:, h * head_dim:(h + 1) * head_dim] for h in range(heads)], axis=0
    )
    row_count = count_ref[row]
    sources = (mine0_ref, mine1_ref, peer0_ref, peer1_ref)
    block_buf[0:BLK] = own_ref[row]
    for slot in range(1, slot_total):
        index = slot_ref[row, slot]
        which = which_ref[row, slot]
        for code, source in enumerate(sources):
            @pl.when(which == code)
            def _(source=source, slot=slot, index=index):
                block_buf[slot * BLK:(slot + 1) * BLK] = source[index]
    blocks = block_buf[...]
    keys = blocks[:, :head_dim]
    values = blocks[:, head_dim:]
    scores = lax.dot_general(
        query, keys, (((1,), (1,)), ((), ())), preferred_element_type=jnp.float32
    )
    key_slot = lax.broadcasted_iota(jnp.int32, (1, slot_total * BLK), 1) // BLK
    scores = jnp.where(key_slot < row_count, scores, NEG_FILL)
    row_max = jnp.max(scores, axis=1, keepdims=True)
    weights = jnp.exp2((scores - row_max) * (score_scale * LOG2_E))
    inverse = 1.0 / jnp.sum(weights, axis=1, keepdims=True)
    probs = (weights * inverse).astype(jnp.bfloat16)
    acc = jnp.dot(probs, values, preferred_element_type=jnp.float32)
    tokens = query_ref.shape[0]
    for h in range(heads):
        out_ref[:, h * head_dim:(h + 1) * head_dim] = acc[h * tokens:(h + 1) * tokens].astype(
            out_ref.dtype
        )


def attend_all(local_queries, column, width, own_blocks, received, slot_index, slot_which,
               row_counts, score_scale):
    seq_rows = local_queries.shape[0]
    qblocks, _, pair_dim = own_blocks.shape
    head_dim = pair_dim // 2
    slot_total = slot_index.shape[1]
    kernel = partial(
        attend_kernel, score_scale=score_scale, slot_total=slot_total, heads=width // head_dim
    )
    whole = lambda shape: pl.BlockSpec(shape, lambda r, s, w, c: (0,) * len(shape))
    return pl.pallas_call(
        kernel,
        out_shape=jax.ShapeDtypeStruct((seq_rows, width), local_queries.dtype),
        grid_spec=pltpu.PrefetchScalarGridSpec(
            num_scalar_prefetch=3,
            grid=(qblocks,),
            in_specs=[
                pl.BlockSpec((BLK, width), lambda r, s, w, c: (r, column)),
                whole(own_blocks.shape),
            ]
            + [whole(part.shape) for part in received],
            out_specs=pl.BlockSpec((BLK, width), lambda r, s, w, c: (r, 0)),
            scratch_shapes=[pltpu.VMEM((slot_total * BLK, pair_dim), own_blocks.dtype)],
        ),
        compiler_params=pltpu.CompilerParams(vmem_limit_bytes=100 * 1024 * 1024),
    )(slot_index, slot_which, row_counts, local_queries, own_blocks, *received)


def make_plan(block_lists, block_counts, group_head, seq_index, shard_count, qblocks, capacity):
    slot_total = block_lists.shape[2]
    entries = qblocks * (slot_total - 1)
    row_lists = lax.dynamic_index_in_dim(block_lists, group_head, 0, keepdims=False)
    row_counts = lax.dynamic_index_in_dim(block_counts, group_head, 0, keepdims=False)
    slot_number = jnp.arange(1, slot_total, dtype=jnp.int32)
    live = (slot_number[None, :] < row_counts[:, None]).reshape(shard_count, entries)
    remote = row_lists[:, 1:].reshape(shard_count, entries)
    owner_shard = remote // qblocks
    within = remote % qblocks
    shard_ids = jnp.arange(shard_count, dtype=jnp.int32)
    hits = ((owner_shard[:, :, None] == shard_ids[None, None, :]) & live[:, :, None]).astype(
        jnp.int32
    )
    place = jnp.sum((jnp.cumsum(hits, axis=1) - hits) * hits, axis=2)
    mine = (live & (owner_shard == seq_index)).astype(jnp.int32)
    slot_match = (place[:, :, None] == jnp.arange(capacity, dtype=jnp.int32)[None, None, :]).astype(
        jnp.int32
    )
    chosen = jnp.sum(mine[:, :, None] * slot_match * within[:, :, None], axis=1)
    my_live = lax.dynamic_index_in_dim(live, seq_index, 0, keepdims=False)
    my_owner = lax.dynamic_index_in_dim(owner_shard, seq_index, 0, keepdims=False)
    my_place = jnp.minimum(lax.dynamic_index_in_dim(place, seq_index, 0, keepdims=False),
                           capacity - 1)
    my_counts = lax.dynamic_slice_in_dim(row_counts, seq_index * qblocks, qblocks, 0)
    return (chosen, my_live, my_owner, my_place, my_counts)


def on_device(queries, keys, values, block_lists, block_counts):
    head_count = lax.axis_size("head")
    shard_count = lax.axis_size("seq")
    head_index = lax.axis_index("head")
    seq_index = lax.axis_index("seq")
    tokens, query_heads, head_dim = queries.shape
    kv_total = keys.shape[1]
    assert head_count == 16 and kv_total == 8
    group_head = (head_index // 8) * 4 + head_index % 4
    half = (head_index // 4) % 2
    seq_rows = tokens * head_count
    qblocks = seq_rows // BLK
    group_size = query_heads // head_count
    slot_total = block_lists.shape[2]
    capacity = (qblocks * (slot_total - 1) + shard_count - 2) // (shard_count - 1)
    assert capacity == 4
    kv = jnp.concatenate([keys, values], axis=2)
    kv = jnp.transpose(kv.reshape(tokens, 2, 1, 4, 2 * head_dim), (1, 2, 3, 0, 4))
    kv = jnp.broadcast_to(kv, (2, 2, 4, tokens, 2 * head_dim))
    kv = kv.reshape(head_count, tokens, 2 * head_dim)
    own_blocks = lax.all_to_all(kv, "head", split_axis=0, concat_axis=0, tiled=True)
    chosen, my_live, my_owner, my_place, my_counts = make_plan(
        block_lists, block_counts, group_head, seq_index, shard_count, qblocks, capacity
    )
    partner = [(h, h ^ 4) for h in range(head_count)]
    mine = []
    peer = []
    for chunk in range(2):
        pick = lax.dynamic_index_in_dim(chosen, 2 * half + chunk, 1, keepdims=False)
        picked = own_blocks[pick]
        if chunk == 1:
            picked, _ = lax.optimization_barrier((picked, mine[0]))
        got = lax.all_to_all(picked, "seq", split_axis=0, concat_axis=0, tiled=True)
        mine.append(got)
        peer.append(lax.ppermute(got, "head", partner))
    spread = jnp.transpose(
        queries.reshape(tokens, 2, 4, 2, group_size, head_dim), (1, 3, 2, 0, 4, 5)
    ).reshape(head_count, tokens, group_size * head_dim)
    spread, _, _ = lax.optimization_barrier((spread, mine[1], peer[0]))
    local_queries = lax.all_to_all(spread, "head", split_axis=0, concat_axis=0, tiled=True)
    local_queries = local_queries.reshape(seq_rows, group_size * head_dim)
    which = jnp.where(my_place // 2 == half, 0, 2) + my_place % 2
    slot_index = jnp.where(my_live, my_owner, 0).reshape(qblocks, slot_total - 1)
    slot_which = jnp.where(my_live, which, 0).reshape(qblocks, slot_total - 1)
    zero_col = jnp.zeros((qblocks, 1), jnp.int32)
    slot_index = jnp.concatenate([zero_col, slot_index], axis=1)
    slot_which = jnp.concatenate([zero_col, slot_which], axis=1)
    score_scale = head_dim ** (-0.5)
    width = group_size * head_dim // 2
    pieces = []
    for column in range(2):
        attended = attend_all(
            local_queries, column, width, own_blocks, mine + peer, slot_index, slot_which,
            my_counts, score_scale
        )
        pieces.append(lax.all_to_all(
            attended.reshape(head_count, tokens, width), "head", split_axis=0, concat_axis=0,
            tiled=True
        ))
    back = jnp.stack(pieces, axis=2)
    back = jnp.transpose(back.reshape(2, 2, 4, tokens, group_size, head_dim), (3, 0, 2, 1, 4, 5))
    return back.reshape(tokens, query_heads, head_dim)


def solution(mesh):
    return jax.shard_map(
        on_device,
        mesh=mesh,
        in_specs=(
            P(("seq", "head"), None, None),
            P(("seq", "head"), None, None),
            P(("seq", "head"), None, None),
            P(),
            P(),
        ),
        out_specs=P(("seq", "head"), None, None),
        check_vma=False,
    )
```

```python
from functools import partial

import jax
import jax.numpy as jnp
from jax import lax
from jax.experimental import pallas as pl
from jax.experimental.pallas import tpu as pltpu
from jax.sharding import PartitionSpec as P

BLK = 128


NEG_FILL = -1e30
LOG2_E = 1.4426950408889634


def attend_kernel(slot_ref, which_ref, count_ref, query_ref, own_ref, mine0_ref, mine1_ref,
                  peer0_ref, peer1_ref, out_ref, block_buf, *, score_scale, slot_total, heads):
    row = pl.program_id(0)
    head_dim = block_buf.shape[1] // 2
    query = query_ref[...]
    query = jnp.concatenate(
        [query[:, h * head_dim:(h + 1) * head_dim] for h in range(heads)], axis=0
    )
    row_count = count_ref[row]
    sources = (mine0_ref, mine1_ref, peer0_ref, peer1_ref)
    block_buf[0:BLK] = own_ref[row]
    for slot in range(1, slot_total):
        index = slot_ref[row, slot]
        which = which_ref[row, slot]
        for code, source in enumerate(sources):
            @pl.when(which == code)
            def _(source=source, slot=slot, index=index):
                block_buf[slot * BLK:(slot + 1) * BLK] = source[index]
    blocks = block_buf[...]
    keys = blocks[:, :head_dim]
    values = blocks[:, head_dim:]
    scores = lax.dot_general(
        query, keys, (((1,), (1,)), ((), ())), preferred_element_type=jnp.float32
    )
    key_slot = lax.broadcasted_iota(jnp.int32, (1, slot_total * BLK), 1) // BLK
    scores = jnp.where(key_slot < row_count, scores, NEG_FILL)
    row_max = jnp.max(scores, axis=1, keepdims=True)
    weights = jnp.exp2((scores - row_max) * (score_scale * LOG2_E))
    inverse = 1.0 / jnp.sum(weights, axis=1, keepdims=True)
    probs = (weights * inverse).astype(jnp.bfloat16)
    acc = jnp.dot(probs, values, preferred_element_type=jnp.float32)
    tokens = query_ref.shape[0]
    for h in range(heads):
        out_ref[:, h * head_dim:(h + 1) * head_dim] = acc[h * tokens:(h + 1) * tokens].astype(
            out_ref.dtype
        )


def attend_all(local_queries, column, width, own_blocks, received, slot_index, slot_which,
               row_counts, score_scale):
    seq_rows = local_queries.shape[0]
    qblocks, _, pair_dim = own_blocks.shape
    head_dim = pair_dim // 2
    slot_total = slot_index.shape[1]
    kernel = partial(
        attend_kernel, score_scale=score_scale, slot_total=slot_total, heads=width // head_dim
    )
    whole = lambda shape: pl.BlockSpec(shape, lambda r, s, w, c: (0,) * len(shape))
    return pl.pallas_call(
        kernel,
        out_shape=jax.ShapeDtypeStruct((seq_rows, width), local_queries.dtype),
        grid_spec=pltpu.PrefetchScalarGridSpec(
            num_scalar_prefetch=3,
            grid=(qblocks,),
            in_specs=[
                pl.BlockSpec((BLK, width), lambda r, s, w, c: (r, column)),
                whole(own_blocks.shape),
            ]
            + [whole(part.shape) for part in received],
            out_specs=pl.BlockSpec((BLK, width), lambda r, s, w, c: (r, 0)),
            scratch_shapes=[pltpu.VMEM((slot_total * BLK, pair_dim), own_blocks.dtype)],
        ),
        compiler_params=pltpu.CompilerParams(vmem_limit_bytes=100 * 1024 * 1024),
    )(slot_index, slot_which, row_counts, local_queries, own_blocks, *received)


def make_plan(block_lists, block_counts, group_head, seq_index, shard_count, qblocks, capacity):
    slot_total = block_lists.shape[2]
    entries = qblocks * (slot_total - 1)
    row_lists = lax.dynamic_index_in_dim(block_lists, group_head, 0, keepdims=False)
    row_counts = lax.dynamic_index_in_dim(block_counts, group_head, 0, keepdims=False)
    slot_number = jnp.arange(1, slot_total, dtype=jnp.int32)
    live = (slot_number[None, :] < row_counts[:, None]).reshape(shard_count, entries)
    remote = row_lists[:, 1:].reshape(shard_count, entries)
    owner_shard = remote // qblocks
    within = remote % qblocks
    shard_ids = jnp.arange(shard_count, dtype=jnp.int32)
    hits = ((owner_shard[:, :, None] == shard_ids[None, None, :]) & live[:, :, None]).astype(
        jnp.int32
    )
    place = jnp.sum((jnp.cumsum(hits, axis=1) - hits) * hits, axis=2)
    mine = (live & (owner_shard == seq_index)).astype(jnp.int32)
    slot_match = (place[:, :, None] == jnp.arange(capacity, dtype=jnp.int32)[None, None, :]).astype(
        jnp.int32
    )
    chosen = jnp.sum(mine[:, :, None] * slot_match * within[:, :, None], axis=1)
    my_live = lax.dynamic_index_in_dim(live, seq_index, 0, keepdims=False)
    my_owner = lax.dynamic_index_in_dim(owner_shard, seq_index, 0, keepdims=False)
    my_place = jnp.minimum(lax.dynamic_index_in_dim(place, seq_index, 0, keepdims=False),
                           capacity - 1)
    my_counts = lax.dynamic_slice_in_dim(row_counts, seq_index * qblocks, qblocks, 0)
    return (chosen, my_live, my_owner, my_place, my_counts)


def on_device(queries, keys, values, block_lists, block_counts):
    head_count = lax.axis_size("head")
    shard_count = lax.axis_size("seq")
    head_index = lax.axis_index("head")
    seq_index = lax.axis_index("seq")
    tokens, query_heads, head_dim = queries.shape
    kv_total = keys.shape[1]
    assert head_count == 16 and kv_total == 8
    group_head = (head_index // 8) * 4 + head_index % 4
    half = (head_index // 4) % 2
    seq_rows = tokens * head_count
    qblocks = seq_rows // BLK
    group_size = query_heads // head_count
    slot_total = block_lists.shape[2]
    capacity = (qblocks * (slot_total - 1) + shard_count - 2) // (shard_count - 1)
    assert capacity == 4
    kv = jnp.concatenate([keys, values], axis=2)
    kv = jnp.transpose(kv.reshape(tokens, 2, 1, 4, 2 * head_dim), (1, 2, 3, 0, 4))
    kv = jnp.broadcast_to(kv, (2, 2, 4, tokens, 2 * head_dim))
    kv = kv.reshape(head_count, tokens, 2 * head_dim)
    own_blocks = lax.all_to_all(kv, "head", split_axis=0, concat_axis=0, tiled=True)
    chosen, my_live, my_owner, my_place, my_counts = make_plan(
        block_lists, block_counts, group_head, seq_index, shard_count, qblocks, capacity
    )
    partner = [(h, h ^ 4) for h in range(head_count)]
    mine = []
    peer = []
    for chunk in range(2):
        pick = lax.dynamic_index_in_dim(chosen, 2 * half + chunk, 1, keepdims=False)
        picked = own_blocks[pick]
        if chunk == 1:
            picked, _ = lax.optimization_barrier((picked, mine[0]))
        got = lax.all_to_all(picked, "seq", split_axis=0, concat_axis=0, tiled=True)
        mine.append(got)
        peer.append(lax.ppermute(got, "head", partner))
    spread = jnp.transpose(
        queries.reshape(tokens, 2, 4, 2, group_size, head_dim), (1, 3, 2, 0, 4, 5)
    ).reshape(head_count, tokens, group_size * head_dim)
    spread, _, _ = lax.optimization_barrier((spread, mine[1], peer[0]))
    local_queries = lax.all_to_all(spread, "head", split_axis=0, concat_axis=0, tiled=True)
    local_queries = local_queries.reshape(seq_rows, group_size * head_dim)
    which = jnp.where(my_place // 2 == half, 0, 2) + my_place % 2
    slot_index = jnp.where(my_live, my_owner, 0).reshape(qblocks, slot_total - 1)
    slot_which = jnp.where(my_live, which, 0).reshape(qblocks, slot_total - 1)
    zero_col = jnp.zeros((qblocks, 1), jnp.int32)
    slot_index = jnp.concatenate([zero_col, slot_index], axis=1)
    slot_which = jnp.concatenate([zero_col, slot_which], axis=1)
    score_scale = head_dim ** (-0.5)
    width = group_size * head_dim
    attended = attend_all(
        local_queries, 0, width, own_blocks, mine + peer, slot_index, slot_which,
        my_counts, score_scale
    )
    back = lax.all_to_all(
        attended.reshape(head_count, tokens, width), "head", split_axis=0, concat_axis=0,
        tiled=True
    )
    back = jnp.transpose(back.reshape(2, 2, 4, tokens, group_size, head_dim), (3, 0, 2, 1, 4, 5))
    return back.reshape(tokens, query_heads, head_dim)


def solution(mesh):
    return jax.shard_map(
        on_device,
        mesh=mesh,
        in_specs=(
            P(("seq", "head"), None, None),
            P(("seq", "head"), None, None),
            P(("seq", "head"), None, None),
            P(),
            P(),
        ),
        out_specs=P(("seq", "head"), None, None),
        check_vma=False,
    )
```

```python
from functools import partial

import jax
import jax.numpy as jnp
from jax import lax
from jax.experimental import pallas as pl
from jax.experimental.pallas import tpu as pltpu
from jax.sharding import PartitionSpec as P

BLK = 128


NEG_FILL = -1e30


def attend_kernel(slot_ref, which_ref, count_ref, query_ref, own_ref, mine0_ref, mine1_ref,
                  peer0_ref, peer1_ref, out_ref, block_buf, *, score_scale, slot_total, heads):
    row = pl.program_id(0)
    head_dim = block_buf.shape[1] // 2
    query = query_ref[...]
    query = jnp.concatenate(
        [query[:, h * head_dim:(h + 1) * head_dim] for h in range(heads)], axis=0
    )
    row_count = count_ref[row]
    sources = (mine0_ref, mine1_ref, peer0_ref, peer1_ref)
    block_buf[0:BLK] = own_ref[row]
    for slot in range(1, slot_total):
        index = slot_ref[row, slot]
        which = which_ref[row, slot]
        for code, source in enumerate(sources):
            @pl.when(which == code)
            def _(source=source, slot=slot, index=index):
                block_buf[slot * BLK:(slot + 1) * BLK] = source[index]
    def attend(masked):
        blocks = block_buf[...]
        keys = blocks[:, :head_dim]
        values = blocks[:, head_dim:]
        scores = lax.dot_general(
            query, keys, (((1,), (1,)), ((), ())), preferred_element_type=jnp.float32
        ) * score_scale
        if masked:
            key_slot = lax.broadcasted_iota(jnp.int32, (1, slot_total * BLK), 1) // BLK
            scores = jnp.where(key_slot < row_count, scores, NEG_FILL)
        row_max = jnp.max(scores, axis=1, keepdims=True)
        weights = jnp.exp(scores - row_max)
        inverse = 1.0 / jnp.sum(weights, axis=1, keepdims=True)
        probs = (weights * inverse).astype(jnp.bfloat16)
        acc = jnp.dot(probs, values, preferred_element_type=jnp.float32)
        tokens = query_ref.shape[0]
        for h in range(heads):
            out_ref[:, h * head_dim:(h + 1) * head_dim] = acc[
                h * tokens:(h + 1) * tokens
            ].astype(out_ref.dtype)

    pl.when(row_count >= slot_total)(lambda: attend(False))
    pl.when(row_count < slot_total)(lambda: attend(True))


def attend_all(local_queries, column, width, own_blocks, received, slot_index, slot_which,
               row_counts, score_scale):
    seq_rows = local_queries.shape[0]
    qblocks, _, pair_dim = own_blocks.shape
    head_dim = pair_dim // 2
    slot_total = slot_index.shape[1]
    kernel = partial(
        attend_kernel, score_scale=score_scale, slot_total=slot_total, heads=width // head_dim
    )
    whole = lambda shape: pl.BlockSpec(shape, lambda r, s, w, c: (0,) * len(shape))
    return pl.pallas_call(
        kernel,
        out_shape=jax.ShapeDtypeStruct((seq_rows, width), local_queries.dtype),
        grid_spec=pltpu.PrefetchScalarGridSpec(
            num_scalar_prefetch=3,
            grid=(qblocks,),
            in_specs=[
                pl.BlockSpec((BLK, width), lambda r, s, w, c: (r, column)),
                whole(own_blocks.shape),
            ]
            + [whole(part.shape) for part in received],
            out_specs=pl.BlockSpec((BLK, width), lambda r, s, w, c: (r, 0)),
            scratch_shapes=[pltpu.VMEM((slot_total * BLK, pair_dim), own_blocks.dtype)],
        ),
        compiler_params=pltpu.CompilerParams(vmem_limit_bytes=100 * 1024 * 1024),
    )(slot_index, slot_which, row_counts, local_queries, own_blocks, *received)


def make_plan(block_lists, block_counts, group_head, seq_index, shard_count, qblocks, capacity):
    slot_total = block_lists.shape[2]
    entries = qblocks * (slot_total - 1)
    row_lists = lax.dynamic_index_in_dim(block_lists, group_head, 0, keepdims=False)
    row_counts = lax.dynamic_index_in_dim(block_counts, group_head, 0, keepdims=False)
    slot_number = jnp.arange(1, slot_total, dtype=jnp.int32)
    live = (slot_number[None, :] < row_counts[:, None]).reshape(shard_count, entries)
    remote = row_lists[:, 1:].reshape(shard_count, entries)
    owner_shard = remote // qblocks
    within = remote % qblocks
    shard_ids = jnp.arange(shard_count, dtype=jnp.int32)
    hits = ((owner_shard[:, :, None] == shard_ids[None, None, :]) & live[:, :, None]).astype(
        jnp.int32
    )
    place = jnp.sum((jnp.cumsum(hits, axis=1) - hits) * hits, axis=2)
    mine = (live & (owner_shard == seq_index)).astype(jnp.int32)
    slot_match = (place[:, :, None] == jnp.arange(capacity, dtype=jnp.int32)[None, None, :]).astype(
        jnp.int32
    )
    chosen = jnp.sum(mine[:, :, None] * slot_match * within[:, :, None], axis=1)
    my_live = lax.dynamic_index_in_dim(live, seq_index, 0, keepdims=False)
    my_owner = lax.dynamic_index_in_dim(owner_shard, seq_index, 0, keepdims=False)
    my_place = jnp.minimum(lax.dynamic_index_in_dim(place, seq_index, 0, keepdims=False),
                           capacity - 1)
    my_counts = lax.dynamic_slice_in_dim(row_counts, seq_index * qblocks, qblocks, 0)
    return (chosen, my_live, my_owner, my_place, my_counts)


def on_device(queries, keys, values, block_lists, block_counts):
    head_count = lax.axis_size("head")
    shard_count = lax.axis_size("seq")
    head_index = lax.axis_index("head")
    seq_index = lax.axis_index("seq")
    tokens, query_heads, head_dim = queries.shape
    kv_total = keys.shape[1]
    assert head_count == 16 and kv_total == 8
    group_head = (head_index // 8) * 4 + head_index % 4
    half = (head_index // 4) % 2
    seq_rows = tokens * head_count
    qblocks = seq_rows // BLK
    group_size = query_heads // head_count
    slot_total = block_lists.shape[2]
    capacity = (qblocks * (slot_total - 1) + shard_count - 2) // (shard_count - 1)
    assert capacity == 4
    kv = jnp.concatenate([keys, values], axis=2)
    kv = jnp.transpose(kv.reshape(tokens, 2, 1, 4, 2 * head_dim), (1, 2, 3, 0, 4))
    kv = jnp.broadcast_to(kv, (2, 2, 4, tokens, 2 * head_dim))
    kv = kv.reshape(head_count, tokens, 2 * head_dim)
    own_blocks = lax.all_to_all(kv, "head", split_axis=0, concat_axis=0, tiled=True)
    chosen, my_live, my_owner, my_place, my_counts = make_plan(
        block_lists, block_counts, group_head, seq_index, shard_count, qblocks, capacity
    )
    partner = [(h, h ^ 4) for h in range(head_count)]
    mine = []
    peer = []
    for chunk in range(2):
        pick = lax.dynamic_index_in_dim(chosen, 2 * half + chunk, 1, keepdims=False)
        picked = own_blocks[pick]
        if chunk == 1:
            picked, _ = lax.optimization_barrier((picked, mine[0]))
        got = lax.all_to_all(picked, "seq", split_axis=0, concat_axis=0, tiled=True)
        mine.append(got)
        peer.append(lax.ppermute(got, "head", partner))
    spread = jnp.transpose(
        queries.reshape(tokens, 2, 4, 2, group_size, head_dim), (1, 3, 2, 0, 4, 5)
    ).reshape(head_count, tokens, group_size * head_dim)
    spread, _, _ = lax.optimization_barrier((spread, mine[1], peer[0]))
    local_queries = lax.all_to_all(spread, "head", split_axis=0, concat_axis=0, tiled=True)
    local_queries = local_queries.reshape(seq_rows, group_size * head_dim)
    which = jnp.where(my_place // 2 == half, 0, 2) + my_place % 2
    slot_index = jnp.where(my_live, my_owner, 0).reshape(qblocks, slot_total - 1)
    slot_which = jnp.where(my_live, which, 0).reshape(qblocks, slot_total - 1)
    zero_col = jnp.zeros((qblocks, 1), jnp.int32)
    slot_index = jnp.concatenate([zero_col, slot_index], axis=1)
    slot_which = jnp.concatenate([zero_col, slot_which], axis=1)
    score_scale = head_dim ** (-0.5)
    width = group_size * head_dim
    attended = attend_all(
        local_queries, 0, width, own_blocks, mine + peer, slot_index, slot_which,
        my_counts, score_scale
    )
    back = lax.all_to_all(
        attended.reshape(head_count, tokens, width), "head", split_axis=0, concat_axis=0,
        tiled=True
    )
    back = jnp.transpose(back.reshape(2, 2, 4, tokens, group_size, head_dim), (3, 0, 2, 1, 4, 5))
    return back.reshape(tokens, query_heads, head_dim)


def solution(mesh):
    return jax.shard_map(
        on_device,
        mesh=mesh,
        in_specs=(
            P(("seq", "head"), None, None),
            P(("seq", "head"), None, None),
            P(("seq", "head"), None, None),
            P(),
            P(),
        ),
        out_specs=P(("seq", "head"), None, None),
        check_vma=False,
    )
```

```python
from functools import partial

import jax
import jax.numpy as jnp
from jax import lax
from jax.experimental import pallas as pl
from jax.experimental.pallas import tpu as pltpu
from jax.sharding import PartitionSpec as P

BLK = 128


NEG_FILL = -1e30


def attend_kernel(slot_ref, which_ref, count_ref, query_ref, own_ref, mine0_ref, mine1_ref,
                  peer0_ref, peer1_ref, out_ref, block_buf, *, score_scale, slot_total, heads):
    row = pl.program_id(0)
    head_dim = block_buf.shape[1] // 2
    query = query_ref[...]
    query = jnp.concatenate(
        [query[:, h * head_dim:(h + 1) * head_dim] for h in range(heads)], axis=0
    )
    row_count = count_ref[row]
    sources = (mine0_ref, mine1_ref, peer0_ref, peer1_ref)
    block_buf[0:BLK] = own_ref[row]
    for slot in range(1, slot_total):
        index = slot_ref[row, slot]
        which = which_ref[row, slot]
        for code, source in enumerate(sources):
            @pl.when(which == code)
            def _(source=source, slot=slot, index=index):
                block_buf[slot * BLK:(slot + 1) * BLK] = source[index]
    blocks = block_buf[...]
    keys = blocks[:, :head_dim]
    values = blocks[:, head_dim:]
    scores = lax.dot_general(
        query, keys, (((1,), (1,)), ((), ())), preferred_element_type=jnp.float32
    ) * score_scale
    key_slot = lax.broadcasted_iota(jnp.int32, (1, slot_total * BLK), 1) // BLK
    scores = jnp.where(key_slot < row_count, scores, NEG_FILL)
    row_max = jnp.max(scores, axis=1, keepdims=True)
    weights = jnp.exp(scores - row_max)
    inverse = 1.0 / jnp.sum(weights, axis=1, keepdims=True)
    probs = (weights * inverse).astype(jnp.bfloat16)
    acc = jnp.dot(probs, values, preferred_element_type=jnp.float32)
    tokens = query_ref.shape[0]
    for h in range(heads):
        out_ref[:, h * head_dim:(h + 1) * head_dim] = acc[h * tokens:(h + 1) * tokens].astype(
            out_ref.dtype
        )


def attend_all(local_queries, column, width, own_blocks, received, slot_index, slot_which,
               row_counts, score_scale):
    seq_rows = local_queries.shape[0]
    qblocks, _, pair_dim = own_blocks.shape
    head_dim = pair_dim // 2
    slot_total = slot_index.shape[1]
    kernel = partial(
        attend_kernel, score_scale=score_scale, slot_total=slot_total, heads=width // head_dim
    )
    whole = lambda shape: pl.BlockSpec(shape, lambda r, s, w, c: (0,) * len(shape))
    return pl.pallas_call(
        kernel,
        out_shape=jax.ShapeDtypeStruct((seq_rows, width), local_queries.dtype),
        grid_spec=pltpu.PrefetchScalarGridSpec(
            num_scalar_prefetch=3,
            grid=(qblocks,),
            in_specs=[
                pl.BlockSpec((BLK, width), lambda r, s, w, c: (r, column)),
                whole(own_blocks.shape),
            ]
            + [whole(part.shape) for part in received],
            out_specs=pl.BlockSpec((BLK, width), lambda r, s, w, c: (r, 0)),
            scratch_shapes=[pltpu.VMEM((slot_total * BLK, pair_dim), own_blocks.dtype)],
        ),
        compiler_params=pltpu.CompilerParams(vmem_limit_bytes=100 * 1024 * 1024),
    )(slot_index, slot_which, row_counts, local_queries, own_blocks, *received)


def make_plan(block_lists, block_counts, group_head, seq_index, shard_count, qblocks, capacity):
    slot_total = block_lists.shape[2]
    entries = qblocks * (slot_total - 1)
    row_lists = lax.dynamic_index_in_dim(block_lists, group_head, 0, keepdims=False)
    row_counts = lax.dynamic_index_in_dim(block_counts, group_head, 0, keepdims=False)
    slot_number = jnp.arange(1, slot_total, dtype=jnp.int32)
    live = (slot_number[None, :] < row_counts[:, None]).reshape(shard_count, entries)
    remote = row_lists[:, 1:].reshape(shard_count, entries)
    owner_shard = remote // qblocks
    within = remote % qblocks
    shard_ids = jnp.arange(shard_count, dtype=jnp.int32)
    hits = ((owner_shard[:, :, None] == shard_ids[None, None, :]) & live[:, :, None]).astype(
        jnp.int32
    )
    place = jnp.sum((jnp.cumsum(hits, axis=1) - hits) * hits, axis=2)
    mine = (live & (owner_shard == seq_index)).astype(jnp.int32)
    slot_match = (place[:, :, None] == jnp.arange(capacity, dtype=jnp.int32)[None, None, :]).astype(
        jnp.int32
    )
    chosen = jnp.sum(mine[:, :, None] * slot_match * within[:, :, None], axis=1)
    my_live = lax.dynamic_index_in_dim(live, seq_index, 0, keepdims=False)
    my_owner = lax.dynamic_index_in_dim(owner_shard, seq_index, 0, keepdims=False)
    my_place = jnp.minimum(lax.dynamic_index_in_dim(place, seq_index, 0, keepdims=False),
                           capacity - 1)
    my_counts = lax.dynamic_slice_in_dim(row_counts, seq_index * qblocks, qblocks, 0)
    return (chosen, my_live, my_owner, my_place, my_counts)


def on_device(queries, keys, values, block_lists, block_counts):
    head_count = lax.axis_size("head")
    shard_count = lax.axis_size("seq")
    head_index = lax.axis_index("head")
    seq_index = lax.axis_index("seq")
    tokens, query_heads, head_dim = queries.shape
    kv_total = keys.shape[1]
    assert head_count == 16 and kv_total == 8
    group_head = (head_index // 8) * 4 + head_index % 4
    half = (head_index // 4) % 2
    seq_rows = tokens * head_count
    qblocks = seq_rows // BLK
    group_size = query_heads // head_count
    slot_total = block_lists.shape[2]
    capacity = (qblocks * (slot_total - 1) + shard_count - 2) // (shard_count - 1)
    assert capacity == 4
    kv = jnp.concatenate([keys, values], axis=2)
    kv = jnp.transpose(kv.reshape(tokens, 2, 1, 4, 2 * head_dim), (1, 2, 3, 0, 4))
    kv = jnp.broadcast_to(kv, (2, 2, 4, tokens, 2 * head_dim))
    kv = kv.reshape(head_count, tokens, 2 * head_dim)
    own_blocks = lax.all_to_all(kv, "head", split_axis=0, concat_axis=0, tiled=True)
    chosen, my_live, my_owner, my_place, my_counts = make_plan(
        block_lists, block_counts, group_head, seq_index, shard_count, qblocks, capacity
    )
    partner = [(h, h ^ 4) for h in range(head_count)]
    mine = []
    peer = []
    for chunk in range(2):
        pick = lax.dynamic_index_in_dim(chosen, 2 * half + chunk, 1, keepdims=False)
        picked = own_blocks[pick]
        if chunk == 1:
            picked, _ = lax.optimization_barrier((picked, mine[0]))
        got = lax.all_to_all(picked, "seq", split_axis=0, concat_axis=0, tiled=True)
        mine.append(got)
        peer.append(lax.ppermute(got, "head", partner))
    spread = jnp.transpose(
        queries.reshape(tokens, 2, 4, 2, group_size, head_dim), (1, 3, 2, 0, 4, 5)
    ).reshape(head_count, tokens, group_size * head_dim)
    spread, _, _ = lax.optimization_barrier((spread, mine[1], peer[0]))
    local_queries = lax.all_to_all(spread, "head", split_axis=0, concat_axis=0, tiled=True)
    local_queries = local_queries.reshape(seq_rows, group_size * head_dim)
    which = jnp.where(my_place // 2 == half, 0, 2) + my_place % 2
    slot_index = jnp.where(my_live, my_owner, 0).reshape(qblocks, slot_total - 1)
    slot_which = jnp.where(my_live, which, 0).reshape(qblocks, slot_total - 1)
    zero_col = jnp.zeros((qblocks, 1), jnp.int32)
    slot_index = jnp.concatenate([zero_col, slot_index], axis=1)
    slot_which = jnp.concatenate([zero_col, slot_which], axis=1)
    score_scale = head_dim ** (-0.5)
    width = group_size * head_dim
    attended = attend_all(
        local_queries, 0, width, own_blocks, mine + peer, slot_index, slot_which,
        my_counts, score_scale
    )
    back = lax.all_to_all(
        attended.reshape(head_count, tokens, width), "head", split_axis=0, concat_axis=0,
        tiled=True
    )
    back = jnp.transpose(back.reshape(2, 2, 4, tokens, group_size * head_dim), (3, 0, 2, 1, 4))
    return back.reshape(tokens, query_heads, head_dim)


def solution(mesh):
    return jax.shard_map(
        on_device,
        mesh=mesh,
        in_specs=(
            P(("seq", "head"), None, None),
            P(("seq", "head"), None, None),
            P(("seq", "head"), None, None),
            P(),
            P(),
        ),
        out_specs=P(("seq", "head"), None, None),
        check_vma=False,
    )
```

```python
from functools import partial

import jax
import jax.numpy as jnp
from jax import lax
from jax.experimental import pallas as pl
from jax.experimental.pallas import tpu as pltpu
from jax.sharding import PartitionSpec as P

BLK = 128


NEG_FILL = -1e30


def attend_kernel(slot_ref, which_ref, count_ref, query_ref, own_ref, mine0_ref, mine1_ref,
                  peer0_ref, peer1_ref, out_ref, block_buf, *, score_scale, slot_total, heads,
                  rows_per_step):
    head_dim = block_buf.shape[1] // 2
    sources = (mine0_ref, mine1_ref, peer0_ref, peer1_ref)
    for sub in range(rows_per_step):
        row = pl.program_id(0) * rows_per_step + sub
        lines = pl.ds(sub * BLK, BLK)
        query = query_ref[lines, :]
        query = jnp.concatenate(
            [query[:, h * head_dim:(h + 1) * head_dim] for h in range(heads)], axis=0
        )
        row_count = count_ref[row]
        block_buf[0:BLK] = own_ref[row]
        for slot in range(1, slot_total):
            index = slot_ref[row, slot]
            which = which_ref[row, slot]
            for code, source in enumerate(sources):
                @pl.when(which == code)
                def _(source=source, slot=slot, index=index):
                    block_buf[slot * BLK:(slot + 1) * BLK] = source[index]
        blocks = block_buf[...]
        keys = blocks[:, :head_dim]
        values = blocks[:, head_dim:]
        scores = lax.dot_general(
            query, keys, (((1,), (1,)), ((), ())), preferred_element_type=jnp.float32
        ) * score_scale
        key_slot = lax.broadcasted_iota(jnp.int32, (1, slot_total * BLK), 1) // BLK
        scores = jnp.where(key_slot < row_count, scores, NEG_FILL)
        row_max = jnp.max(scores, axis=1, keepdims=True)
        weights = jnp.exp(scores - row_max)
        inverse = 1.0 / jnp.sum(weights, axis=1, keepdims=True)
        probs = (weights * inverse).astype(jnp.bfloat16)
        acc = jnp.dot(probs, values, preferred_element_type=jnp.float32)
        for h in range(heads):
            out_ref[lines, h * head_dim:(h + 1) * head_dim] = acc[
                h * BLK:(h + 1) * BLK
            ].astype(out_ref.dtype)


def attend_all(local_queries, column, width, own_blocks, received, slot_index, slot_which,
               row_counts, score_scale):
    seq_rows = local_queries.shape[0]
    qblocks, _, pair_dim = own_blocks.shape
    head_dim = pair_dim // 2
    slot_total = slot_index.shape[1]
    rows_per_step = 2
    kernel = partial(
        attend_kernel, score_scale=score_scale, slot_total=slot_total, heads=width // head_dim,
        rows_per_step=rows_per_step
    )
    whole = lambda shape: pl.BlockSpec(shape, lambda r, s, w, c: (0,) * len(shape))
    return pl.pallas_call(
        kernel,
        out_shape=jax.ShapeDtypeStruct((seq_rows, width), local_queries.dtype),
        grid_spec=pltpu.PrefetchScalarGridSpec(
            num_scalar_prefetch=3,
            grid=(qblocks // rows_per_step,),
            in_specs=[
                pl.BlockSpec((rows_per_step * BLK, width), lambda r, s, w, c: (r, column)),
                whole(own_blocks.shape),
            ]
            + [whole(part.shape) for part in received],
            out_specs=pl.BlockSpec((rows_per_step * BLK, width), lambda r, s, w, c: (r, 0)),
            scratch_shapes=[pltpu.VMEM((slot_total * BLK, pair_dim), own_blocks.dtype)],
        ),
        compiler_params=pltpu.CompilerParams(vmem_limit_bytes=100 * 1024 * 1024),
    )(slot_index, slot_which, row_counts, local_queries, own_blocks, *received)


def make_plan(block_lists, block_counts, group_head, seq_index, shard_count, qblocks, capacity):
    slot_total = block_lists.shape[2]
    entries = qblocks * (slot_total - 1)
    row_lists = lax.dynamic_index_in_dim(block_lists, group_head, 0, keepdims=False)
    row_counts = lax.dynamic_index_in_dim(block_counts, group_head, 0, keepdims=False)
    slot_number = jnp.arange(1, slot_total, dtype=jnp.int32)
    live = (slot_number[None, :] < row_counts[:, None]).reshape(shard_count, entries)
    remote = row_lists[:, 1:].reshape(shard_count, entries)
    owner_shard = remote // qblocks
    within = remote % qblocks
    shard_ids = jnp.arange(shard_count, dtype=jnp.int32)
    hits = ((owner_shard[:, :, None] == shard_ids[None, None, :]) & live[:, :, None]).astype(
        jnp.int32
    )
    place = jnp.sum((jnp.cumsum(hits, axis=1) - hits) * hits, axis=2)
    mine = (live & (owner_shard == seq_index)).astype(jnp.int32)
    slot_match = (place[:, :, None] == jnp.arange(capacity, dtype=jnp.int32)[None, None, :]).astype(
        jnp.int32
    )
    chosen = jnp.sum(mine[:, :, None] * slot_match * within[:, :, None], axis=1)
    my_live = lax.dynamic_index_in_dim(live, seq_index, 0, keepdims=False)
    my_owner = lax.dynamic_index_in_dim(owner_shard, seq_index, 0, keepdims=False)
    my_place = jnp.minimum(lax.dynamic_index_in_dim(place, seq_index, 0, keepdims=False),
                           capacity - 1)
    my_counts = lax.dynamic_slice_in_dim(row_counts, seq_index * qblocks, qblocks, 0)
    return (chosen, my_live, my_owner, my_place, my_counts)


def on_device(queries, keys, values, block_lists, block_counts):
    head_count = lax.axis_size("head")
    shard_count = lax.axis_size("seq")
    head_index = lax.axis_index("head")
    seq_index = lax.axis_index("seq")
    tokens, query_heads, head_dim = queries.shape
    kv_total = keys.shape[1]
    assert head_count == 16 and kv_total == 8
    group_head = (head_index // 8) * 4 + head_index % 4
    half = (head_index // 4) % 2
    seq_rows = tokens * head_count
    qblocks = seq_rows // BLK
    group_size = query_heads // head_count
    slot_total = block_lists.shape[2]
    capacity = (qblocks * (slot_total - 1) + shard_count - 2) // (shard_count - 1)
    assert capacity == 4
    kv = jnp.concatenate([keys, values], axis=2)
    kv = jnp.transpose(kv.reshape(tokens, 2, 1, 4, 2 * head_dim), (1, 2, 3, 0, 4))
    kv = jnp.broadcast_to(kv, (2, 2, 4, tokens, 2 * head_dim))
    kv = kv.reshape(head_count, tokens, 2 * head_dim)
    own_blocks = lax.all_to_all(kv, "head", split_axis=0, concat_axis=0, tiled=True)
    chosen, my_live, my_owner, my_place, my_counts = make_plan(
        block_lists, block_counts, group_head, seq_index, shard_count, qblocks, capacity
    )
    partner = [(h, h ^ 4) for h in range(head_count)]
    mine = []
    peer = []
    for chunk in range(2):
        pick = lax.dynamic_index_in_dim(chosen, 2 * half + chunk, 1, keepdims=False)
        picked = own_blocks[pick]
        if chunk == 1:
            picked, _ = lax.optimization_barrier((picked, mine[0]))
        got = lax.all_to_all(picked, "seq", split_axis=0, concat_axis=0, tiled=True)
        mine.append(got)
        peer.append(lax.ppermute(got, "head", partner))
    spread = jnp.transpose(
        queries.reshape(tokens, 2, 4, 2, group_size, head_dim), (1, 3, 2, 0, 4, 5)
    ).reshape(head_count, tokens, group_size * head_dim)
    spread, _, _ = lax.optimization_barrier((spread, mine[1], peer[0]))
    local_queries = lax.all_to_all(spread, "head", split_axis=0, concat_axis=0, tiled=True)
    local_queries = local_queries.reshape(seq_rows, group_size * head_dim)
    which = jnp.where(my_place // 2 == half, 0, 2) + my_place % 2
    slot_index = jnp.where(my_live, my_owner, 0).reshape(qblocks, slot_total - 1)
    slot_which = jnp.where(my_live, which, 0).reshape(qblocks, slot_total - 1)
    zero_col = jnp.zeros((qblocks, 1), jnp.int32)
    slot_index = jnp.concatenate([zero_col, slot_index], axis=1)
    slot_which = jnp.concatenate([zero_col, slot_which], axis=1)
    score_scale = head_dim ** (-0.5)
    width = group_size * head_dim
    attended = attend_all(
        local_queries, 0, width, own_blocks, mine + peer, slot_index, slot_which,
        my_counts, score_scale
    )
    back = lax.all_to_all(
        attended.reshape(head_count, tokens, width), "head", split_axis=0, concat_axis=0,
        tiled=True
    )
    back = jnp.transpose(back.reshape(2, 2, 4, tokens, group_size * head_dim), (3, 0, 2, 1, 4))
    return back.reshape(tokens, query_heads, head_dim)


def solution(mesh):
    return jax.shard_map(
        on_device,
        mesh=mesh,
        in_specs=(
            P(("seq", "head"), None, None),
            P(("seq", "head"), None, None),
            P(("seq", "head"), None, None),
            P(),
            P(),
        ),
        out_specs=P(("seq", "head"), None, None),
        check_vma=False,
    )
```

```python
from functools import partial

import jax
import jax.numpy as jnp
from jax import lax
from jax.experimental import pallas as pl
from jax.experimental.pallas import tpu as pltpu
from jax.sharding import PartitionSpec as P

BLK = 128


NEG_FILL = -1e30


def attend_kernel(slot_ref, which_ref, count_ref, query_ref, own_ref, mine0_ref, mine1_ref,
                  peer0_ref, peer1_ref, out_ref, block_buf, *, score_scale, slot_total, heads,
                  rows_per_step):
    head_dim = block_buf.shape[1] // 2
    sources = (mine0_ref, mine1_ref, peer0_ref, peer1_ref)
    for sub in range(rows_per_step):
        row = pl.program_id(0) * rows_per_step + sub
        lines = pl.ds(sub * BLK, BLK)
        query = query_ref[lines, :]
        query = jnp.concatenate(
            [query[:, h * head_dim:(h + 1) * head_dim] for h in range(heads)], axis=0
        )
        row_count = count_ref[row]
        block_buf[0:BLK] = own_ref[row]
        for slot in range(1, slot_total):
            index = slot_ref[row, slot]
            which = which_ref[row, slot]
            for code, source in enumerate(sources):
                @pl.when(which == code)
                def _(source=source, slot=slot, index=index):
                    block_buf[slot * BLK:(slot + 1) * BLK] = source[index]
        blocks = block_buf[...]
        keys = blocks[:, :head_dim]
        values = blocks[:, head_dim:]
        scores = lax.dot_general(
            query, keys, (((1,), (1,)), ((), ())), preferred_element_type=jnp.float32
        ) * score_scale
        key_slot = lax.broadcasted_iota(jnp.int32, (1, slot_total * BLK), 1) // BLK
        scores = jnp.where(key_slot < row_count, scores, NEG_FILL)
        row_max = jnp.max(scores, axis=1, keepdims=True)
        weights = jnp.exp(scores - row_max)
        inverse = 1.0 / jnp.sum(weights, axis=1, keepdims=True)
        probs = (weights * inverse).astype(jnp.bfloat16)
        acc = jnp.dot(probs, values, preferred_element_type=jnp.float32)
        for h in range(heads):
            out_ref[lines, h * head_dim:(h + 1) * head_dim] = acc[
                h * BLK:(h + 1) * BLK
            ].astype(out_ref.dtype)


def attend_all(local_queries, column, width, own_blocks, received, slot_index, slot_which,
               row_counts, score_scale):
    seq_rows = local_queries.shape[0]
    qblocks, _, pair_dim = own_blocks.shape
    head_dim = pair_dim // 2
    slot_total = slot_index.shape[1]
    rows_per_step = 4
    kernel = partial(
        attend_kernel, score_scale=score_scale, slot_total=slot_total, heads=width // head_dim,
        rows_per_step=rows_per_step
    )
    whole = lambda shape: pl.BlockSpec(shape, lambda r, s, w, c: (0,) * len(shape))
    return pl.pallas_call(
        kernel,
        out_shape=jax.ShapeDtypeStruct((seq_rows, width), local_queries.dtype),
        grid_spec=pltpu.PrefetchScalarGridSpec(
            num_scalar_prefetch=3,
            grid=(qblocks // rows_per_step,),
            in_specs=[
                pl.BlockSpec((rows_per_step * BLK, width), lambda r, s, w, c: (r, column)),
                whole(own_blocks.shape),
            ]
            + [whole(part.shape) for part in received],
            out_specs=pl.BlockSpec((rows_per_step * BLK, width), lambda r, s, w, c: (r, 0)),
            scratch_shapes=[pltpu.VMEM((slot_total * BLK, pair_dim), own_blocks.dtype)],
        ),
        compiler_params=pltpu.CompilerParams(vmem_limit_bytes=100 * 1024 * 1024),
    )(slot_index, slot_which, row_counts, local_queries, own_blocks, *received)


def make_plan(block_lists, block_counts, group_head, seq_index, shard_count, qblocks, capacity):
    slot_total = block_lists.shape[2]
    entries = qblocks * (slot_total - 1)
    row_lists = lax.dynamic_index_in_dim(block_lists, group_head, 0, keepdims=False)
    row_counts = lax.dynamic_index_in_dim(block_counts, group_head, 0, keepdims=False)
    slot_number = jnp.arange(1, slot_total, dtype=jnp.int32)
    live = (slot_number[None, :] < row_counts[:, None]).reshape(shard_count, entries)
    remote = row_lists[:, 1:].reshape(shard_count, entries)
    owner_shard = remote // qblocks
    within = remote % qblocks
    shard_ids = jnp.arange(shard_count, dtype=jnp.int32)
    hits = ((owner_shard[:, :, None] == shard_ids[None, None, :]) & live[:, :, None]).astype(
        jnp.int32
    )
    place = jnp.sum((jnp.cumsum(hits, axis=1) - hits) * hits, axis=2)
    mine = (live & (owner_shard == seq_index)).astype(jnp.int32)
    slot_match = (place[:, :, None] == jnp.arange(capacity, dtype=jnp.int32)[None, None, :]).astype(
        jnp.int32
    )
    chosen = jnp.sum(mine[:, :, None] * slot_match * within[:, :, None], axis=1)
    my_live = lax.dynamic_index_in_dim(live, seq_index, 0, keepdims=False)
    my_owner = lax.dynamic_index_in_dim(owner_shard, seq_index, 0, keepdims=False)
    my_place = jnp.minimum(lax.dynamic_index_in_dim(place, seq_index, 0, keepdims=False),
                           capacity - 1)
    my_counts = lax.dynamic_slice_in_dim(row_counts, seq_index * qblocks, qblocks, 0)
    return (chosen, my_live, my_owner, my_place, my_counts)


def on_device(queries, keys, values, block_lists, block_counts):
    head_count = lax.axis_size("head")
    shard_count = lax.axis_size("seq")
    head_index = lax.axis_index("head")
    seq_index = lax.axis_index("seq")
    tokens, query_heads, head_dim = queries.shape
    kv_total = keys.shape[1]
    assert head_count == 16 and kv_total == 8
    group_head = (head_index // 8) * 4 + head_index % 4
    half = (head_index // 4) % 2
    seq_rows = tokens * head_count
    qblocks = seq_rows // BLK
    group_size = query_heads // head_count
    slot_total = block_lists.shape[2]
    capacity = (qblocks * (slot_total - 1) + shard_count - 2) // (shard_count - 1)
    assert capacity == 4
    kv = jnp.concatenate([keys, values], axis=2)
    kv = jnp.transpose(kv.reshape(tokens, 2, 1, 4, 2 * head_dim), (1, 2, 3, 0, 4))
    kv = jnp.broadcast_to(kv, (2, 2, 4, tokens, 2 * head_dim))
    kv = kv.reshape(head_count, tokens, 2 * head_dim)
    own_blocks = lax.all_to_all(kv, "head", split_axis=0, concat_axis=0, tiled=True)
    chosen, my_live, my_owner, my_place, my_counts = make_plan(
        block_lists, block_counts, group_head, seq_index, shard_count, qblocks, capacity
    )
    partner = [(h, h ^ 4) for h in range(head_count)]
    mine = []
    peer = []
    for chunk in range(2):
        pick = lax.dynamic_index_in_dim(chosen, 2 * half + chunk, 1, keepdims=False)
        picked = own_blocks[pick]
        if chunk == 1:
            picked, _ = lax.optimization_barrier((picked, mine[0]))
        got = lax.all_to_all(picked, "seq", split_axis=0, concat_axis=0, tiled=True)
        mine.append(got)
        peer.append(lax.ppermute(got, "head", partner))
    spread = jnp.transpose(
        queries.reshape(tokens, 2, 4, 2, group_size, head_dim), (1, 3, 2, 0, 4, 5)
    ).reshape(head_count, tokens, group_size * head_dim)
    spread, _, _ = lax.optimization_barrier((spread, mine[1], peer[0]))
    local_queries = lax.all_to_all(spread, "head", split_axis=0, concat_axis=0, tiled=True)
    local_queries = local_queries.reshape(seq_rows, group_size * head_dim)
    which = jnp.where(my_place // 2 == half, 0, 2) + my_place % 2
    slot_index = jnp.where(my_live, my_owner, 0).reshape(qblocks, slot_total - 1)
    slot_which = jnp.where(my_live, which, 0).reshape(qblocks, slot_total - 1)
    zero_col = jnp.zeros((qblocks, 1), jnp.int32)
    slot_index = jnp.concatenate([zero_col, slot_index], axis=1)
    slot_which = jnp.concatenate([zero_col, slot_which], axis=1)
    score_scale = head_dim ** (-0.5)
    width = group_size * head_dim
    attended = attend_all(
        local_queries, 0, width, own_blocks, mine + peer, slot_index, slot_which,
        my_counts, score_scale
    )
    back = lax.all_to_all(
        attended.reshape(head_count, tokens, width), "head", split_axis=0, concat_axis=0,
        tiled=True
    )
    back = jnp.transpose(back.reshape(2, 2, 4, tokens, group_size * head_dim), (3, 0, 2, 1, 4))
    return back.reshape(tokens, query_heads, head_dim)


def solution(mesh):
    return jax.shard_map(
        on_device,
        mesh=mesh,
        in_specs=(
            P(("seq", "head"), None, None),
            P(("seq", "head"), None, None),
            P(("seq", "head"), None, None),
            P(),
            P(),
        ),
        out_specs=P(("seq", "head"), None, None),
        check_vma=False,
    )
```
